128 devices in a mesh: prow: 8 (over z, core), pcol: 16 (over x, y).
Axes of the slice: x: 4, y: 4, z: 4, core: 2. Of those that a mesh axis runs over, the one named last changes fastest.
Arguments:
- front: float32 [4, 8, 512, 2, 16, 512], P(None, 'prow', None, None, 'pcol'), as said below
- child_block: float32 [2, 8, 512, 1, 16, 512], P(None, 'prow', None, None, 'pcol'), as said below
- child_to_parent: int32 [8192], replicated, may hold values from 0 to 16383, as said below
Outputs:
- front_out: float32 [4, 8, 512, 2, 16, 512], P(None, 'prow', None, None, 'pcol')
The draws below stay inside these ranges and needn't reach their ends.
Inputs may be any that keep to these rules, and one draw needn't show every extreme that they name: `child_to_parent`: all entries are distinct. Child indices come in groups of 32 consecutive positions of one grid row's local order that share a destination. The child indices held by one grid row (row blocks congruent to it modulo 8) send at most 256 of them to the parent row blocks of any one grid row, and those held by one grid column at most 64 to the parent column blocks of any one grid column; both bounds are reached in every draw. `front`: Symmetric. `child_block`: Symmetric.
All inputs are finite; a program needn't handle non-finite values.
Results may differ from the reference program's by a relative error of at most 0.0001.
Values sent between devices are 32-bit elements; how exact they have to be, the bound alone decides.
No kernel may reach another device: no remote copies, remote signals or barrier semaphores. Data moves between devices by JAX's collectives and lax.ppermute only.
A program may use at most 192 MiB of HBM per device.

```python
import jax
import jax.numpy as jnp
from jax import lax

F = 16384
NB = 512
CB = 8192
NP = 2
SB = 32
PROWS = 8
PCOLS = 16
RB = 4
CBK = 2
CRB = 2
CCB = 1


def symmetric_draw(key, order, spread, diag_low, diag_high):
    key_noise, key_diag = jax.random.split(key)
    noise = jax.random.normal(key_noise, (order, order), jnp.float32)
    scaled = (noise + noise.T) * (spread * 0.70710678 / order ** 0.5)
    diag_vals = jax.random.uniform(key_diag, (order,), jnp.float32, diag_low, diag_high)
    row_ids = jnp.arange(order, dtype=jnp.int32)
    return jnp.where(row_ids[:, None] == row_ids[None, :], diag_vals[:, None], scaled)


def draw_front(key, part):
    full = symmetric_draw(jax.random.fold_in(key, 3), F, 1.5, 6.0, 8.0)
    return full.reshape(RB, PROWS, NB, CBK, PCOLS, NB)


def draw_child_block(key, part):
    full = symmetric_draw(jax.random.fold_in(key, 5), CB, 1.0, -0.5, 0.5)
    return full.reshape(CRB, PROWS, NB, CCB, PCOLS, NB)


def draw_child_to_parent(key, part):
    key_shift, key_start, key_perm = jax.random.split(jax.random.fold_in(key, 7), 3)
    pair_size = PCOLS // PROWS
    half_rows = PROWS // 2
    indices = jnp.arange(CB, dtype=jnp.int32)
    which_block = indices // NB
    source = which_block % PROWS
    local_row = which_block // PROWS * NB + indices % NB
    sub_block = local_row // SB
    pair_index = sub_block // pair_size
    side_index = sub_block % pair_size
    is_heavy = pair_index % half_rows == 0
    row_shift = jax.random.randint(key_shift, (), 0, PROWS, dtype=jnp.int32)
    row_start = jax.random.randint(key_start, (PROWS,), 0, PROWS - 1, dtype=jnp.int32)
    home_row = (source + row_shift) % PROWS
    light_order = pair_index // half_rows * (half_rows - 1) + pair_index % half_rows - 1
    light_row = (home_row + 1 + (row_start[source] + light_order) % (PROWS - 1)) % PROWS
    target_row = jnp.where(is_heavy, home_row, light_row)
    target_col = target_row + PROWS * side_index
    one_hot = (target_col[:, None] == jnp.arange(PCOLS, dtype=jnp.int32)[None, :]).astype(jnp.int32)
    slot_rank = jnp.sum(jnp.cumsum(one_hot, axis=0) * one_hot, axis=1) - 1
    col_span = F // PCOLS
    perm_keys = jax.random.split(key_perm, PCOLS)
    shuffles = jax.vmap(lambda subkey: jax.random.permutation(subkey, col_span))(perm_keys).astype(jnp.int32)
    col_ids = jnp.arange(PCOLS, dtype=jnp.int32)
    wanted = jnp.where(col_ids == PCOLS - 1, col_span - 1, 0).astype(jnp.int32)
    found_at = jnp.argmax(shuffles == wanted[:, None], axis=1)
    leading = shuffles[:, 0]
    shuffles = shuffles.at[col_ids, found_at].set(leading).at[col_ids, 0].set(wanted)
    position = shuffles[target_col, slot_rank]
    return ((position // NB * PCOLS + target_col) * NB + position % NB).astype(jnp.int32)


def setup_inputs(seed: int = 0) -> dict:
    splits = jax.random.split(jax.random.key(seed), 4)
    return {
        "front": draw_front(jax.random.fold_in(splits[3], 71), 0),
        "child_block": draw_child_block(jax.random.fold_in(splits[3], 71), 0),
        "child_to_parent": draw_child_to_parent(jax.random.fold_in(splits[3], 71), 0),
    }


def reference(front, child_block, child_to_parent):
    matrix = front.reshape(F, F)
    child = child_block.reshape(CB, CB)
    matrix = matrix.at[child_to_parent[:, None], child_to_parent[None, :]].add(child)
    for panel_id in range(NP):
        first_row = panel_id * NB
        next_row = first_row + NB
        low_factor = jnp.linalg.cholesky(matrix[first_row:next_row, first_row:next_row])
        below = jax.scipy.linalg.solve_triangular(low_factor, matrix[next_row:, first_row:next_row].T, lower=True).T
        update = jnp.dot(below, below.T, precision=lax.Precision.HIGHEST)
        matrix = matrix.at[next_row:, next_row:].set(matrix[next_row:, next_row:] - update)
        panel_block = jnp.concatenate([jnp.zeros((first_row, NB), jnp.float32), low_factor, below], axis=0)
        matrix = matrix.at[:, first_row:next_row].set(panel_block)
    return matrix.reshape(front.shape)
```

```python
import jax
import jax.numpy as jnp
from jax import lax
from jax.sharding import PartitionSpec as P

NP = 2


HIGHEST = lax.Precision.HIGHEST


def from_root(x, axis, root):
    mine = lax.axis_index(axis) == root
    return lax.psum(jnp.where(mine, x, jnp.zeros_like(x)), axis)


def slot_ranks(destiny, groups):
    one_hot = (destiny[:, :, None] == jnp.arange(groups, dtype=jnp.int32)[None, None, :]).astype(
        jnp.int32
    )
    return jnp.sum(jnp.cumsum(one_hot, axis=1) * one_hot, axis=2) - 1


def by_source(values, blocks_local, groups, block_width):
    return jnp.transpose(values.reshape(blocks_local, groups, block_width), (1, 0, 2)).reshape(
        groups, blocks_local * block_width
    )


def route_tables(mapping, blocks_local, groups, block_width, my_index, capacity, parent_len):
    local_len = blocks_local * block_width
    parent_blk = mapping // block_width
    dest_group = by_source(parent_blk % groups, blocks_local, groups, block_width)
    parent_pos = by_source(
        parent_blk // groups * block_width + mapping % block_width,
        blocks_local,
        groups,
        block_width,
    )
    slot_rank = slot_ranks(dest_group, groups)
    own_dest = lax.dynamic_index_in_dim(dest_group, my_index, 0, keepdims=False)
    own_slot = lax.dynamic_index_in_dim(slot_rank, my_index, 0, keepdims=False)
    send_pick = (
        jnp.full((groups * capacity,), local_len, jnp.int32)
        .at[own_dest * capacity + own_slot]
        .set(jnp.arange(local_len, dtype=jnp.int32))
    )
    flat_slot = jnp.arange(groups, dtype=jnp.int32)[:, None] * capacity + slot_rank
    landing = jnp.where(dest_group == my_index, parent_pos, parent_len)
    recv_pick = (
        jnp.full((parent_len,), groups * capacity, jnp.int32)
        .at[landing.reshape(-1)]
        .set(flat_slot.reshape(-1), mode="drop")
    )
    return (send_pick, recv_pick)


def factor_block(block_in, tile_size):
    order_len = block_in.shape[0]
    num_tiles = order_len // tile_size
    identity = jnp.eye(tile_size, dtype=jnp.float32)
    zero_tile = jnp.zeros((tile_size, tile_size), jnp.float32)
    low_tiles = [[zero_tile for col_tile in range(num_tiles)] for row_tile in range(num_tiles)]
    diag_inverses = []
    working = block_in
    for col_tile in range(num_tiles):
        tile_start = col_tile * tile_size
        tile_end = tile_start + tile_size
        diag_tile = jnp.linalg.cholesky(working[tile_start:tile_end, tile_start:tile_end])
        diag_inverse = jax.scipy.linalg.solve_triangular(diag_tile, identity, lower=True)
        low_tiles[col_tile][col_tile] = diag_tile
        diag_inverses.append(diag_inverse)
        if tile_end < order_len:
            stripe_rows = jnp.dot(
                working[tile_end:, tile_start:tile_end], diag_inverse.T, precision=HIGHEST
            )
            for row_tile in range(col_tile + 1, num_tiles):
                offset = (row_tile - col_tile - 1) * tile_size
                low_tiles[row_tile][col_tile] = stripe_rows[offset : offset + tile_size]
            working = working.at[tile_end:, tile_end:].add(
                -jnp.dot(stripe_rows, stripe_rows.T, precision=HIGHEST)
            )
    inv_tiles = [[zero_tile for col_tile in range(num_tiles)] for row_tile in range(num_tiles)]
    for row_tile in range(num_tiles):
        inv_tiles[row_tile][row_tile] = diag_inverses[row_tile]
        for col_tile in range(row_tile - 1, -1, -1):
            partial_sum = zero_tile
            for mid_tile in range(col_tile, row_tile):
                partial_sum = partial_sum + jnp.dot(
                    low_tiles[row_tile][mid_tile], inv_tiles[mid_tile][col_tile], precision=HIGHEST
                )
            inv_tiles[row_tile][col_tile] = -jnp.dot(
                diag_inverses[row_tile], partial_sum, precision=HIGHEST
            )
    return (jnp.block(low_tiles), jnp.block(inv_tiles))


def local(front, child_block, child_to_parent):
    grid_rows = lax.axis_size("prow")
    grid_cols = lax.axis_size("pcol")
    my_row = lax.axis_index("prow")
    my_col = lax.axis_index("pcol")
    row_blocks = front.shape[0]
    block_width = front.shape[2]
    col_blocks = front.shape[3]
    child_rblocks = child_block.shape[0]
    child_cblocks = child_block.shape[3]
    local_rows = row_blocks * block_width
    local_cols = col_blocks * block_width
    child_rows = child_rblocks * block_width
    child_cols = child_cblocks * block_width
    cap_rows = 2 * child_rows // grid_rows
    cap_cols = 2 * child_cols // grid_cols
    tile_size = min(64, block_width)
    row_send, row_recv = route_tables(
        child_to_parent, child_rblocks, grid_rows, block_width, my_row, cap_rows, local_rows
    )
    col_send, col_recv = route_tables(
        child_to_parent, child_cblocks, grid_cols, block_width, my_col, cap_cols, local_cols
    )
    padded = jnp.pad(child_block.reshape(child_rows, child_cols), ((0, 1), (0, 1)))
    moved = jnp.take(jnp.take(padded, row_send, axis=0), col_send, axis=1).reshape(
        grid_rows, cap_rows, grid_cols, cap_cols
    )
    moved = lax.all_to_all(
        lax.all_to_all(moved, "prow", split_axis=0, concat_axis=0, tiled=True),
        "pcol",
        split_axis=2,
        concat_axis=2,
        tiled=True,
    )
    arrived = jnp.pad(moved.reshape(grid_rows * cap_rows, grid_cols * cap_cols), ((0, 1), (0, 1)))
    added = jnp.take(jnp.take(arrived, row_recv, axis=0), col_recv, axis=1)
    matrix = front.reshape(local_rows, local_cols) + added
    panel = NP * block_width
    row_blk = jnp.repeat(jnp.arange(row_blocks, dtype=jnp.int32) * grid_rows + my_row, block_width)
    col_blk = jnp.repeat(jnp.arange(col_blocks, dtype=jnp.int32) * grid_cols + my_col, block_width)
    first_cols = matrix[:, :block_width]
    first_rows = matrix[:block_width, :]
    zero_cols = jnp.zeros_like(first_cols)
    zero_rows = jnp.zeros_like(first_rows)
    x_part = jnp.concatenate(
        [jnp.where(my_col == p, first_cols, zero_cols) for p in range(NP)], axis=1
    )
    y_part = jnp.concatenate(
        [jnp.where(my_row == p, first_rows, zero_rows) for p in range(NP)], axis=0
    )
    corner = first_rows[:, :block_width]
    zero_corner = jnp.zeros_like(corner)
    d_part = jnp.concatenate(
        [
            jnp.concatenate(
                [
                    jnp.where((my_row == p) & (my_col == q), corner, zero_corner)
                    for q in range(NP)
                ],
                axis=1,
            )
            for p in range(NP)
        ],
        axis=0,
    )
    x_full = lax.psum(x_part, "pcol")
    y_full = lax.psum(y_part, "prow")
    d_full = lax.psum(d_part, ("prow", "pcol"))
    low = jnp.tril(jnp.linalg.cholesky(d_full))
    low_inv = jax.scipy.linalg.solve_triangular(
        low, jnp.eye(panel, dtype=jnp.float32), lower=True
    )
    rows_f = jnp.dot(x_full, low_inv.T, precision=HIGHEST)
    cols_f = lax.dot_general(
        y_full, low_inv, (((0,), (1,)), ((), ())), precision=HIGHEST
    )
    low_rows = lax.dynamic_slice_in_dim(low, jnp.minimum(my_row, NP - 1) * block_width, block_width, 0)
    head = jnp.where(my_row < NP, low_rows, rows_f[:block_width])
    rows_f = jnp.concatenate([head, rows_f[block_width:]], axis=0)
    lane = jnp.arange(panel, dtype=jnp.int32)[None, :]
    keep_row = (row_blk[:, None] >= NP) | (lane < (row_blk[:, None] * block_width))
    rows_u = jnp.where(keep_row, rows_f, 0.0)
    cols_u = jnp.where((col_blk >= NP)[:, None], cols_f, 0.0)
    matrix = matrix - jnp.dot(rows_u, cols_u.T, precision=HIGHEST)
    out_first = matrix[:, :block_width]
    for p in range(NP):
        out_first = jnp.where(
            my_col == p, rows_f[:, p * block_width : (p + 1) * block_width], out_first
        )
    matrix = jnp.concatenate([out_first, matrix[:, block_width:]], axis=1)
    return matrix.reshape(front.shape)


def solution(mesh):
    in_specs = (
        P(None, "prow", None, None, "pcol", None),
        P(None, "prow", None, None, "pcol", None),
        P(),
    )
    out_specs = P(None, "prow", None, None, "pcol", None)
    return jax.shard_map(local, mesh=mesh, in_specs=in_specs, out_specs=out_specs, check_vma=False)
```

```python
import jax
import jax.numpy as jnp
from jax import lax
from jax.sharding import PartitionSpec as P

NP = 2


HIGHEST = lax.Precision.HIGHEST


def from_root(x, axis, root):
    mine = lax.axis_index(axis) == root
    return lax.psum(jnp.where(mine, x, jnp.zeros_like(x)), axis)


def slot_ranks(destiny, groups):
    one_hot = (destiny[:, :, None] == jnp.arange(groups, dtype=jnp.int32)[None, None, :]).astype(
        jnp.int32
    )
    return jnp.sum(jnp.cumsum(one_hot, axis=1) * one_hot, axis=2) - 1


def by_source(values, blocks_local, groups, block_width):
    return jnp.transpose(values.reshape(blocks_local, groups, block_width), (1, 0, 2)).reshape(
        groups, blocks_local * block_width
    )


def route_tables(mapping, blocks_local, groups, block_width, my_index, capacity, parent_len):
    local_len = blocks_local * block_width
    parent_blk = mapping // block_width
    dest_group = by_source(parent_blk % groups, blocks_local, groups, block_width)
    parent_pos = by_source(
        parent_blk // groups * block_width + mapping % block_width,
        blocks_local,
        groups,
        block_width,
    )
    slot_rank = slot_ranks(dest_group, groups)
    own_dest = lax.dynamic_index_in_dim(dest_group, my_index, 0, keepdims=False)
    own_slot = lax.dynamic_index_in_dim(slot_rank, my_index, 0, keepdims=False)
    send_pick = (
        jnp.full((groups * capacity,), local_len, jnp.int32)
        .at[own_dest * capacity + own_slot]
        .set(jnp.arange(local_len, dtype=jnp.int32))
    )
    flat_slot = jnp.arange(groups, dtype=jnp.int32)[:, None] * capacity + slot_rank
    landing = jnp.where(dest_group == my_index, parent_pos, parent_len)
    recv_pick = (
        jnp.full((parent_len,), groups * capacity, jnp.int32)
        .at[landing.reshape(-1)]
        .set(flat_slot.reshape(-1), mode="drop")
    )
    return (send_pick, recv_pick)


def factor_block(block_in, tile_size):
    order_len = block_in.shape[0]
    num_tiles = order_len // tile_size
    identity = jnp.eye(tile_size, dtype=jnp.float32)
    zero_tile = jnp.zeros((tile_size, tile_size), jnp.float32)
    low_tiles = [[zero_tile for col_tile in range(num_tiles)] for row_tile in range(num_tiles)]
    diag_inverses = []
    working = block_in
    for col_tile in range(num_tiles):
        tile_start = col_tile * tile_size
        tile_end = tile_start + tile_size
        diag_tile = jnp.linalg.cholesky(working[tile_start:tile_end, tile_start:tile_end])
        diag_inverse = jax.scipy.linalg.solve_triangular(diag_tile, identity, lower=True)
        low_tiles[col_tile][col_tile] = diag_tile
        diag_inverses.append(diag_inverse)
        if tile_end < order_len:
            stripe_rows = jnp.dot(
                working[tile_end:, tile_start:tile_end], diag_inverse.T, precision=HIGHEST
            )
            for row_tile in range(col_tile + 1, num_tiles):
                offset = (row_tile - col_tile - 1) * tile_size
                low_tiles[row_tile][col_tile] = stripe_rows[offset : offset + tile_size]
            working = working.at[tile_end:, tile_end:].add(
                -jnp.dot(stripe_rows, stripe_rows.T, precision=HIGHEST)
            )
    inv_tiles = [[zero_tile for col_tile in range(num_tiles)] for row_tile in range(num_tiles)]
    for row_tile in range(num_tiles):
        inv_tiles[row_tile][row_tile] = diag_inverses[row_tile]
        for col_tile in range(row_tile - 1, -1, -1):
            partial_sum = zero_tile
            for mid_tile in range(col_tile, row_tile):
                partial_sum = partial_sum + jnp.dot(
                    low_tiles[row_tile][mid_tile], inv_tiles[mid_tile][col_tile], precision=HIGHEST
                )
            inv_tiles[row_tile][col_tile] = -jnp.dot(
                diag_inverses[row_tile], partial_sum, precision=HIGHEST
            )
    return (jnp.block(low_tiles), jnp.block(inv_tiles))


def local(front, child_block, child_to_parent):
    grid_rows = lax.axis_size("prow")
    grid_cols = lax.axis_size("pcol")
    my_row = lax.axis_index("prow")
    my_col = lax.axis_index("pcol")
    row_blocks = front.shape[0]
    block_width = front.shape[2]
    col_blocks = front.shape[3]
    child_rblocks = child_block.shape[0]
    child_cblocks = child_block.shape[3]
    local_rows = row_blocks * block_width
    local_cols = col_blocks * block_width
    child_rows = child_rblocks * block_width
    child_cols = child_cblocks * block_width
    cap_rows = 2 * child_rows // grid_rows
    cap_cols = 2 * child_cols // grid_cols
    tile_size = min(64, block_width)
    row_send, row_recv = route_tables(
        child_to_parent, child_rblocks, grid_rows, block_width, my_row, cap_rows, local_rows
    )
    col_send, col_recv = route_tables(
        child_to_parent, child_cblocks, grid_cols, block_width, my_col, cap_cols, local_cols
    )
    child_local = child_block.reshape(child_rows, child_cols)
    staged = jnp.take(jnp.pad(child_local, ((0, 0), (0, 1))), col_send, axis=1)
    staged = lax.all_to_all(
        staged.reshape(child_rows, grid_cols, cap_cols), "pcol", split_axis=1, concat_axis=1, tiled=True
    ).reshape(child_rows, grid_cols * cap_cols)
    moved = jnp.take(jnp.pad(staged, ((0, 1), (0, 0))), row_send, axis=0)
    moved = lax.all_to_all(
        moved.reshape(grid_rows, cap_rows, grid_cols * cap_cols), "prow", split_axis=0, concat_axis=0, tiled=True
    )
    arrived = jnp.pad(moved.reshape(grid_rows * cap_rows, grid_cols * cap_cols), ((0, 1), (0, 1)))
    added = jnp.take(jnp.take(arrived, row_recv, axis=0), col_recv, axis=1)
    matrix = front.reshape(local_rows, local_cols) + added
    panel = NP * block_width
    row_blk = jnp.repeat(jnp.arange(row_blocks, dtype=jnp.int32) * grid_rows + my_row, block_width)
    col_blk = jnp.repeat(jnp.arange(col_blocks, dtype=jnp.int32) * grid_cols + my_col, block_width)
    first_cols = matrix[:, :block_width]
    first_rows = matrix[:block_width, :]
    zero_cols = jnp.zeros_like(first_cols)
    zero_rows = jnp.zeros_like(first_rows)
    x_part = jnp.concatenate(
        [jnp.where(my_col == p, first_cols, zero_cols) for p in range(NP)], axis=1
    )
    y_part = jnp.concatenate(
        [jnp.where(my_row == p, first_rows, zero_rows) for p in range(NP)], axis=0
    )
    panel_ids = jnp.arange(panel, dtype=jnp.int32)
    child_row_ids = (
        (jnp.arange(child_rblocks, dtype=jnp.int32)[:, None] * grid_rows + my_row) * block_width
        + jnp.arange(block_width, dtype=jnp.int32)[None, :]
    ).reshape(-1)
    child_col_ids = (
        (jnp.arange(child_cblocks, dtype=jnp.int32)[:, None] * grid_cols + my_col) * block_width
        + jnp.arange(block_width, dtype=jnp.int32)[None, :]
    ).reshape(-1)
    row_hit = (child_to_parent[child_row_ids][None, :] == panel_ids[:, None]).astype(jnp.float32)
    col_hit = (child_to_parent[child_col_ids][None, :] == panel_ids[:, None]).astype(jnp.float32)
    corner_child = jnp.dot(
        jnp.dot(row_hit, child_local, precision=HIGHEST), col_hit.T, precision=HIGHEST
    )
    corner = front.reshape(local_rows, local_cols)[:block_width, :block_width]
    zero_corner = jnp.zeros_like(corner)
    d_part = corner_child + jnp.concatenate(
        [
            jnp.concatenate(
                [
                    jnp.where((my_row == p) & (my_col == q), corner, zero_corner)
                    for q in range(NP)
                ],
                axis=1,
            )
            for p in range(NP)
        ],
        axis=0,
    )
    x_full = lax.psum(x_part, "pcol")
    y_full = lax.psum(y_part, "prow")
    d_full = lax.psum(d_part, ("prow", "pcol"))
    low = jnp.tril(jnp.linalg.cholesky(d_full))
    low_inv = jax.scipy.linalg.solve_triangular(
        low, jnp.eye(panel, dtype=jnp.float32), lower=True
    )
    rows_f = jnp.dot(x_full, low_inv.T, precision=HIGHEST)
    cols_f = lax.dot_general(
        y_full, low_inv, (((0,), (1,)), ((), ())), precision=HIGHEST
    )
    low_rows = lax.dynamic_slice_in_dim(low, jnp.minimum(my_row, NP - 1) * block_width, block_width, 0)
    head = jnp.where(my_row < NP, low_rows, rows_f[:block_width])
    rows_f = jnp.concatenate([head, rows_f[block_width:]], axis=0)
    lane = jnp.arange(panel, dtype=jnp.int32)[None, :]
    keep_row = (row_blk[:, None] >= NP) | (lane < (row_blk[:, None] * block_width))
    rows_u = jnp.where(keep_row, rows_f, 0.0)
    cols_u = jnp.where((col_blk >= NP)[:, None], cols_f, 0.0)
    matrix = matrix - jnp.dot(rows_u, cols_u.T, precision=HIGHEST)
    out_first = matrix[:, :block_width]
    for p in range(NP):
        out_first = jnp.where(
            my_col == p, rows_f[:, p * block_width : (p + 1) * block_width], out_first
        )
    matrix = jnp.concatenate([out_first, matrix[:, block_width:]], axis=1)
    return matrix.reshape(front.shape)


def solution(mesh):
    in_specs = (
        P(None, "prow", None, None, "pcol", None),
        P(None, "prow", None, None, "pcol", None),
        P(),
    )
    out_specs = P(None, "prow", None, None, "pcol", None)
    return jax.shard_map(local, mesh=mesh, in_specs=in_specs, out_specs=out_specs, check_vma=False)
```

```python
import jax
import jax.numpy as jnp
from jax import lax
from jax.sharding import PartitionSpec as P

NP = 2
SB = 32


HIGHEST = lax.Precision.HIGHEST


def from_root(x, axis, root):
    mine = lax.axis_index(axis) == root
    return lax.psum(jnp.where(mine, x, jnp.zeros_like(x)), axis)


def slot_ranks(destiny, groups):
    one_hot = (destiny[:, :, None] == jnp.arange(groups, dtype=jnp.int32)[None, None, :]).astype(
        jnp.int32
    )
    return jnp.sum(jnp.cumsum(one_hot, axis=1) * one_hot, axis=2) - 1


def by_source(values, blocks_local, groups, block_width):
    return jnp.transpose(values.reshape(blocks_local, groups, block_width), (1, 0, 2)).reshape(
        groups, blocks_local * block_width
    )


def route_tables(mapping, blocks_local, groups, block_width, my_index, capacity, parent_len):
    local_len = blocks_local * block_width
    num_groups = local_len // SB
    group_slots = capacity // SB
    src_map = by_source(mapping, blocks_local, groups, block_width)
    dest_g = (src_map[:, ::SB] // block_width) % groups
    rank_g = slot_ranks(dest_g, groups)
    group_ids = jnp.arange(num_groups, dtype=jnp.int32)
    lane = jnp.arange(SB, dtype=jnp.int32)
    own_dest = lax.dynamic_index_in_dim(dest_g, my_index, 0, keepdims=False)
    own_rank = lax.dynamic_index_in_dim(rank_g, my_index, 0, keepdims=False)
    slot_ids = jnp.arange(groups * group_slots, dtype=jnp.int32)
    hit = (own_dest[None, :] == (slot_ids // group_slots)[:, None]) & (
        own_rank[None, :] == (slot_ids % group_slots)[:, None]
    )
    picked = jnp.sum(jnp.where(hit, group_ids[None, :], 0), axis=1)
    send_pick = jnp.where(
        jnp.any(hit, axis=1)[:, None], picked[:, None] * SB + lane[None, :], local_len
    ).reshape(-1)
    hit_in = (dest_g[:, None, :] == my_index) & (
        rank_g[:, None, :] == jnp.arange(group_slots, dtype=jnp.int32)[None, :, None]
    )
    picked_in = jnp.sum(jnp.where(hit_in, group_ids[None, None, :], 0), axis=2)
    elem = (picked_in[:, :, None] * SB + lane[None, None, :]).reshape(groups, capacity)
    parent_of_slot = jnp.take_along_axis(src_map, elem, axis=1)
    parent_blk = parent_of_slot // block_width
    landing = parent_blk // groups * block_width + parent_of_slot % block_width
    valid = jnp.repeat(jnp.any(hit_in, axis=2), SB, axis=1)
    landing = jnp.where(valid, landing, parent_len).reshape(-1)
    match = landing[None, :] == jnp.arange(parent_len, dtype=jnp.int32)[:, None]
    recv_pick = jnp.where(
        jnp.any(match, axis=1), jnp.argmax(match, axis=1).astype(jnp.int32), groups * capacity
    )
    return (send_pick, recv_pick)


def factor_block(block_in, tile_size):
    order_len = block_in.shape[0]
    num_tiles = order_len // tile_size
    identity = jnp.eye(tile_size, dtype=jnp.float32)
    zero_tile = jnp.zeros((tile_size, tile_size), jnp.float32)
    low_tiles = [[zero_tile for col_tile in range(num_tiles)] for row_tile in range(num_tiles)]
    diag_inverses = []
    working = block_in
    for col_tile in range(num_tiles):
        tile_start = col_tile * tile_size
        tile_end = tile_start + tile_size
        diag_tile = jnp.linalg.cholesky(working[tile_start:tile_end, tile_start:tile_end])
        diag_inverse = jax.scipy.linalg.solve_triangular(diag_tile, identity, lower=True)
        low_tiles[col_tile][col_tile] = diag_tile
        diag_inverses.append(diag_inverse)
        if tile_end < order_len:
            stripe_rows = jnp.dot(
                working[tile_end:, tile_start:tile_end], diag_inverse.T, precision=HIGHEST
            )
            for row_tile in range(col_tile + 1, num_tiles):
                offset = (row_tile - col_tile - 1) * tile_size
                low_tiles[row_tile][col_tile] = stripe_rows[offset : offset + tile_size]
            working = working.at[tile_end:, tile_end:].add(
                -jnp.dot(stripe_rows, stripe_rows.T, precision=HIGHEST)
            )
    inv_tiles = [[zero_tile for col_tile in range(num_tiles)] for row_tile in range(num_tiles)]
    for row_tile in range(num_tiles):
        inv_tiles[row_tile][row_tile] = diag_inverses[row_tile]
        for col_tile in range(row_tile - 1, -1, -1):
            partial_sum = zero_tile
            for mid_tile in range(col_tile, row_tile):
                partial_sum = partial_sum + jnp.dot(
                    low_tiles[row_tile][mid_tile], inv_tiles[mid_tile][col_tile], precision=HIGHEST
                )
            inv_tiles[row_tile][col_tile] = -jnp.dot(
                diag_inverses[row_tile], partial_sum, precision=HIGHEST
            )
    return (jnp.block(low_tiles), jnp.block(inv_tiles))


def local(front, child_block, child_to_parent):
    grid_rows = lax.axis_size("prow")
    grid_cols = lax.axis_size("pcol")
    my_row = lax.axis_index("prow")
    my_col = lax.axis_index("pcol")
    row_blocks = front.shape[0]
    block_width = front.shape[2]
    col_blocks = front.shape[3]
    child_rblocks = child_block.shape[0]
    child_cblocks = child_block.shape[3]
    local_rows = row_blocks * block_width
    local_cols = col_blocks * block_width
    child_rows = child_rblocks * block_width
    child_cols = child_cblocks * block_width
    cap_rows = 2 * child_rows // grid_rows
    cap_cols = 2 * child_cols // grid_cols
    tile_size = min(64, block_width)
    row_send, row_recv = route_tables(
        child_to_parent, child_rblocks, grid_rows, block_width, my_row, cap_rows, local_rows
    )
    col_send, col_recv = route_tables(
        child_to_parent, child_cblocks, grid_cols, block_width, my_col, cap_cols, local_cols
    )
    child_local = child_block.reshape(child_rows, child_cols)
    staged = jnp.take(jnp.pad(child_local, ((0, 0), (0, 1))), col_send, axis=1)
    staged = lax.all_to_all(
        staged.reshape(child_rows, grid_cols, cap_cols), "pcol", split_axis=1, concat_axis=1, tiled=True
    ).reshape(child_rows, grid_cols * cap_cols)
    moved = jnp.take(jnp.pad(staged, ((0, 1), (0, 0))), row_send, axis=0)
    moved = lax.all_to_all(
        moved.reshape(grid_rows, cap_rows, grid_cols * cap_cols), "prow", split_axis=0, concat_axis=0, tiled=True
    )
    arrived = jnp.pad(moved.reshape(grid_rows * cap_rows, grid_cols * cap_cols), ((0, 1), (0, 1)))
    added = jnp.take(jnp.take(arrived, row_recv, axis=0), col_recv, axis=1)
    matrix = front.reshape(local_rows, local_cols) + added
    panel = NP * block_width
    row_blk = jnp.repeat(jnp.arange(row_blocks, dtype=jnp.int32) * grid_rows + my_row, block_width)
    col_blk = jnp.repeat(jnp.arange(col_blocks, dtype=jnp.int32) * grid_cols + my_col, block_width)
    first_cols = matrix[:, :block_width]
    first_rows = matrix[:block_width, :]
    zero_cols = jnp.zeros_like(first_cols)
    zero_rows = jnp.zeros_like(first_rows)
    x_part = jnp.concatenate(
        [jnp.where(my_col == p, first_cols, zero_cols) for p in range(NP)], axis=1
    )
    y_part = jnp.concatenate(
        [jnp.where(my_row == p, first_rows, zero_rows) for p in range(NP)], axis=0
    )
    panel_ids = jnp.arange(panel, dtype=jnp.int32)
    child_row_ids = (
        (jnp.arange(child_rblocks, dtype=jnp.int32)[:, None] * grid_rows + my_row) * block_width
        + jnp.arange(block_width, dtype=jnp.int32)[None, :]
    ).reshape(-1)
    child_col_ids = (
        (jnp.arange(child_cblocks, dtype=jnp.int32)[:, None] * grid_cols + my_col) * block_width
        + jnp.arange(block_width, dtype=jnp.int32)[None, :]
    ).reshape(-1)
    row_hit = (child_to_parent[child_row_ids][None, :] == panel_ids[:, None]).astype(jnp.float32)
    col_hit = (child_to_parent[child_col_ids][None, :] == panel_ids[:, None]).astype(jnp.float32)
    corner_child = jnp.dot(
        jnp.dot(row_hit, child_local, precision=HIGHEST), col_hit.T, precision=HIGHEST
    )
    corner = front.reshape(local_rows, local_cols)[:block_width, :block_width]
    zero_corner = jnp.zeros_like(corner)
    d_part = corner_child + jnp.concatenate(
        [
            jnp.concatenate(
                [
                    jnp.where((my_row == p) & (my_col == q), corner, zero_corner)
                    for q in range(NP)
                ],
                axis=1,
            )
            for p in range(NP)
        ],
        axis=0,
    )
    x_full = lax.psum(x_part, "pcol")
    y_full = lax.psum(y_part, "prow")
    d_full = lax.psum(d_part, ("prow", "pcol"))
    low = jnp.tril(jnp.linalg.cholesky(d_full))
    low_inv = jax.scipy.linalg.solve_triangular(
        low, jnp.eye(panel, dtype=jnp.float32), lower=True
    )
    rows_f = jnp.dot(x_full, low_inv.T, precision=HIGHEST)
    cols_f = lax.dot_general(
        y_full, low_inv, (((0,), (1,)), ((), ())), precision=HIGHEST
    )
    low_rows = lax.dynamic_slice_in_dim(low, jnp.minimum(my_row, NP - 1) * block_width, block_width, 0)
    head = jnp.where(my_row < NP, low_rows, rows_f[:block_width])
    rows_f = jnp.concatenate([head, rows_f[block_width:]], axis=0)
    lane = jnp.arange(panel, dtype=jnp.int32)[None, :]
    keep_row = (row_blk[:, None] >= NP) | (lane < (row_blk[:, None] * block_width))
    rows_u = jnp.where(keep_row, rows_f, 0.0)
    cols_u = jnp.where((col_blk >= NP)[:, None], cols_f, 0.0)
    matrix = matrix - jnp.dot(rows_u, cols_u.T, precision=HIGHEST)
    out_first = matrix[:, :block_width]
    for p in range(NP):
        out_first = jnp.where(
            my_col == p, rows_f[:, p * block_width : (p + 1) * block_width], out_first
        )
    matrix = jnp.concatenate([out_first, matrix[:, block_width:]], axis=1)
    return matrix.reshape(front.shape)


def solution(mesh):
    in_specs = (
        P(None, "prow", None, None, "pcol", None),
        P(None, "prow", None, None, "pcol", None),
        P(),
    )
    out_specs = P(None, "prow", None, None, "pcol", None)
    return jax.shard_map(local, mesh=mesh, in_specs=in_specs, out_specs=out_specs, check_vma=False)
```

```python
import jax
import jax.numpy as jnp
from jax import lax
from jax.sharding import PartitionSpec as P

NP = 2
SB = 32


HIGHEST = lax.Precision.HIGHEST


def from_root(x, axis, root):
    mine = lax.axis_index(axis) == root
    return lax.psum(jnp.where(mine, x, jnp.zeros_like(x)), axis)


def slot_ranks(destiny, groups):
    one_hot = (destiny[:, :, None] == jnp.arange(groups, dtype=jnp.int32)[None, None, :]).astype(
        jnp.int32
    )
    return jnp.sum(jnp.cumsum(one_hot, axis=1) * one_hot, axis=2) - 1


def by_source(values, blocks_local, groups, block_width):
    return jnp.transpose(values.reshape(blocks_local, groups, block_width), (1, 0, 2)).reshape(
        groups, blocks_local * block_width
    )


def route_tables(mapping, blocks_local, groups, block_width, my_index, capacity, parent_len):
    local_len = blocks_local * block_width
    num_groups = local_len // SB
    group_slots = capacity // SB
    src_map = by_source(mapping, blocks_local, groups, block_width)
    dest_g = (src_map[:, ::SB] // block_width) % groups
    rank_g = slot_ranks(dest_g, groups)
    group_ids = jnp.arange(num_groups, dtype=jnp.int32)
    lane = jnp.arange(SB, dtype=jnp.int32)
    own_dest = lax.dynamic_index_in_dim(dest_g, my_index, 0, keepdims=False)
    own_rank = lax.dynamic_index_in_dim(rank_g, my_index, 0, keepdims=False)
    slot_ids = jnp.arange(groups * group_slots, dtype=jnp.int32)
    hit = (own_dest[None, :] == (slot_ids // group_slots)[:, None]) & (
        own_rank[None, :] == (slot_ids % group_slots)[:, None]
    )
    picked = jnp.sum(jnp.where(hit, group_ids[None, :], 0), axis=1)
    send_pick = jnp.where(
        jnp.any(hit, axis=1)[:, None], picked[:, None] * SB + lane[None, :], local_len
    ).reshape(-1)
    hit_in = (dest_g[:, None, :] == my_index) & (
        rank_g[:, None, :] == jnp.arange(group_slots, dtype=jnp.int32)[None, :, None]
    )
    picked_in = jnp.sum(jnp.where(hit_in, group_ids[None, None, :], 0), axis=2)
    elem = (picked_in[:, :, None] * SB + lane[None, None, :]).reshape(groups, capacity)
    parent_of_slot = jnp.take_along_axis(src_map, elem, axis=1)
    parent_blk = parent_of_slot // block_width
    landing = parent_blk // groups * block_width + parent_of_slot % block_width
    valid = jnp.repeat(jnp.any(hit_in, axis=2), SB, axis=1)
    landing = jnp.where(valid, landing, parent_len).reshape(-1)
    match = landing[None, :] == jnp.arange(parent_len, dtype=jnp.int32)[:, None]
    recv_pick = jnp.where(
        jnp.any(match, axis=1), jnp.argmax(match, axis=1).astype(jnp.int32), groups * capacity
    )
    return (send_pick, recv_pick)


def factor_block(block_in, tile_size):
    order_len = block_in.shape[0]
    num_tiles = order_len // tile_size
    identity = jnp.eye(tile_size, dtype=jnp.float32)
    zero_tile = jnp.zeros((tile_size, tile_size), jnp.float32)
    low_tiles = [[zero_tile for col_tile in range(num_tiles)] for row_tile in range(num_tiles)]
    diag_inverses = []
    working = block_in
    for col_tile in range(num_tiles):
        tile_start = col_tile * tile_size
        tile_end = tile_start + tile_size
        diag_tile = jnp.linalg.cholesky(working[tile_start:tile_end, tile_start:tile_end])
        diag_inverse = jax.scipy.linalg.solve_triangular(diag_tile, identity, lower=True)
        low_tiles[col_tile][col_tile] = diag_tile
        diag_inverses.append(diag_inverse)
        if tile_end < order_len:
            stripe_rows = jnp.dot(
                working[tile_end:, tile_start:tile_end], diag_inverse.T, precision=HIGHEST
            )
            for row_tile in range(col_tile + 1, num_tiles):
                offset = (row_tile - col_tile - 1) * tile_size
                low_tiles[row_tile][col_tile] = stripe_rows[offset : offset + tile_size]
            working = working.at[tile_end:, tile_end:].add(
                -jnp.dot(stripe_rows, stripe_rows.T, precision=HIGHEST)
            )
    inv_tiles = [[zero_tile for col_tile in range(num_tiles)] for row_tile in range(num_tiles)]
    for row_tile in range(num_tiles):
        inv_tiles[row_tile][row_tile] = diag_inverses[row_tile]
        for col_tile in range(row_tile - 1, -1, -1):
            partial_sum = zero_tile
            for mid_tile in range(col_tile, row_tile):
                partial_sum = partial_sum + jnp.dot(
                    low_tiles[row_tile][mid_tile], inv_tiles[mid_tile][col_tile], precision=HIGHEST
                )
            inv_tiles[row_tile][col_tile] = -jnp.dot(
                diag_inverses[row_tile], partial_sum, precision=HIGHEST
            )
    return (jnp.block(low_tiles), jnp.block(inv_tiles))


def local(front, child_block, child_to_parent):
    grid_rows = lax.axis_size("prow")
    grid_cols = lax.axis_size("pcol")
    my_row = lax.axis_index("prow")
    my_col = lax.axis_index("pcol")
    row_blocks = front.shape[0]
    block_width = front.shape[2]
    col_blocks = front.shape[3]
    child_rblocks = child_block.shape[0]
    child_cblocks = child_block.shape[3]
    local_rows = row_blocks * block_width
    local_cols = col_blocks * block_width
    child_rows = child_rblocks * block_width
    child_cols = child_cblocks * block_width
    cap_rows = 2 * child_rows // grid_rows
    cap_cols = 2 * child_cols // grid_cols
    tile_size = min(64, block_width)
    row_send, row_recv = route_tables(
        child_to_parent, child_rblocks, grid_rows, block_width, my_row, cap_rows, local_rows
    )
    col_send, col_recv = route_tables(
        child_to_parent, child_cblocks, grid_cols, block_width, my_col, cap_cols, local_cols
    )
    child_local = child_block.reshape(child_rows, child_cols)
    staged = jnp.take(jnp.pad(child_local, ((0, 0), (0, 1))), col_send, axis=1)
    staged = lax.all_to_all(
        staged.reshape(child_rows, grid_cols, cap_cols), "pcol", split_axis=1, concat_axis=1, tiled=True
    ).reshape(child_rows, grid_cols * cap_cols)
    moved = jnp.take(jnp.pad(staged, ((0, 1), (0, 0))), row_send, axis=0)
    moved = lax.all_to_all(
        moved.reshape(grid_rows, cap_rows, grid_cols * cap_cols), "prow", split_axis=0, concat_axis=0, tiled=True
    )
    arrived = jnp.pad(moved.reshape(grid_rows * cap_rows, grid_cols * cap_cols), ((0, 1), (0, 1)))
    added = jnp.take(jnp.take(arrived, row_recv, axis=0), col_recv, axis=1)
    matrix = front.reshape(local_rows, local_cols) + added
    panel = NP * block_width
    row_blk = jnp.repeat(jnp.arange(row_blocks, dtype=jnp.int32) * grid_rows + my_row, block_width)
    col_blk = jnp.repeat(jnp.arange(col_blocks, dtype=jnp.int32) * grid_cols + my_col, block_width)
    first_cols = matrix[:, :block_width]
    first_rows = matrix[:block_width, :]
    zero_cols = jnp.zeros_like(first_cols)
    zero_rows = jnp.zeros_like(first_rows)
    x_part = jnp.concatenate(
        [jnp.where(my_col == p, first_cols, zero_cols) for p in range(NP)], axis=1
    )
    y_part = jnp.concatenate(
        [jnp.where(my_row == p, first_rows, zero_rows) for p in range(NP)], axis=0
    )
    panel_ids = jnp.arange(panel, dtype=jnp.int32)
    child_row_ids = (
        (jnp.arange(child_rblocks, dtype=jnp.int32)[:, None] * grid_rows + my_row) * block_width
        + jnp.arange(block_width, dtype=jnp.int32)[None, :]
    ).reshape(-1)
    child_col_ids = (
        (jnp.arange(child_cblocks, dtype=jnp.int32)[:, None] * grid_cols + my_col) * block_width
        + jnp.arange(block_width, dtype=jnp.int32)[None, :]
    ).reshape(-1)
    row_hit = (child_to_parent[child_row_ids][None, :] == panel_ids[:, None]).astype(jnp.float32)
    col_hit = (child_to_parent[child_col_ids][None, :] == panel_ids[:, None]).astype(jnp.float32)
    corner_child = jnp.dot(
        jnp.dot(row_hit, child_local, precision=HIGHEST), col_hit.T, precision=HIGHEST
    )
    corner = front[0, 0, :, 0, 0, :]
    zero_corner = jnp.zeros_like(corner)
    d_part = corner_child + jnp.concatenate(
        [
            jnp.concatenate(
                [
                    jnp.where((my_row == p) & (my_col == q), corner, zero_corner)
                    for q in range(NP)
                ],
                axis=1,
            )
            for p in range(NP)
        ],
        axis=0,
    )
    d_full = lax.psum(d_part, ("prow", "pcol"))
    d_full, x_part, y_part = lax.optimization_barrier((d_full, x_part, y_part))
    x_full = lax.psum(x_part, "pcol")
    y_full = lax.psum(y_part, "prow")
    low = jnp.tril(jnp.linalg.cholesky(d_full))
    low_inv = jax.scipy.linalg.solve_triangular(
        low, jnp.eye(panel, dtype=jnp.float32), lower=True
    )
    rows_f = jnp.dot(x_full, low_inv.T, precision=HIGHEST)
    cols_f = lax.dot_general(
        y_full, low_inv, (((0,), (1,)), ((), ())), precision=HIGHEST
    )
    low_rows = lax.dynamic_slice_in_dim(low, jnp.minimum(my_row, NP - 1) * block_width, block_width, 0)
    head = jnp.where(my_row < NP, low_rows, rows_f[:block_width])
    rows_f = jnp.concatenate([head, rows_f[block_width:]], axis=0)
    lane = jnp.arange(panel, dtype=jnp.int32)[None, :]
    keep_row = (row_blk[:, None] >= NP) | (lane < (row_blk[:, None] * block_width))
    rows_u = jnp.where(keep_row, rows_f, 0.0)
    cols_u = jnp.where((col_blk >= NP)[:, None], cols_f, 0.0)
    matrix = matrix - jnp.dot(rows_u, cols_u.T, precision=HIGHEST)
    out_first = matrix[:, :block_width]
    for p in range(NP):
        out_first = jnp.where(
            my_col == p, rows_f[:, p * block_width : (p + 1) * block_width], out_first
        )
    matrix = jnp.concatenate([out_first, matrix[:, block_width:]], axis=1)
    return matrix.reshape(front.shape)


def solution(mesh):
    in_specs = (
        P(None, "prow", None, None, "pcol", None),
        P(None, "prow", None, None, "pcol", None),
        P(),
    )
    out_specs = P(None, "prow", None, None, "pcol", None)
    return jax.shard_map(local, mesh=mesh, in_specs=in_specs, out_specs=out_specs, check_vma=False)
```

```python
import jax
import jax.numpy as jnp
from jax import lax
from jax.sharding import PartitionSpec as P

NP = 2
SB = 32


HIGHEST = lax.Precision.HIGHEST


def from_root(x, axis, root):
    mine = lax.axis_index(axis) == root
    return lax.psum(jnp.where(mine, x, jnp.zeros_like(x)), axis)


def slot_ranks(destiny, groups):
    one_hot = (destiny[:, :, None] == jnp.arange(groups, dtype=jnp.int32)[None, None, :]).astype(
        jnp.int32
    )
    return jnp.sum(jnp.cumsum(one_hot, axis=1) * one_hot, axis=2) - 1


def by_source(values, blocks_local, groups, block_width):
    return jnp.transpose(values.reshape(blocks_local, groups, block_width), (1, 0, 2)).reshape(
        groups, blocks_local * block_width
    )


def route_tables(mapping, blocks_local, groups, block_width, my_index, capacity, parent_len):
    local_len = blocks_local * block_width
    num_groups = local_len // SB
    group_slots = capacity // SB
    src_map = by_source(mapping, blocks_local, groups, block_width)
    dest_g = (src_map[:, ::SB] // block_width) % groups
    rank_g = slot_ranks(dest_g, groups)
    group_ids = jnp.arange(num_groups, dtype=jnp.int32)
    lane = jnp.arange(SB, dtype=jnp.int32)
    own_dest = lax.dynamic_index_in_dim(dest_g, my_index, 0, keepdims=False)
    own_rank = lax.dynamic_index_in_dim(rank_g, my_index, 0, keepdims=False)
    slot_ids = jnp.arange(groups * group_slots, dtype=jnp.int32)
    hit = (own_dest[None, :] == (slot_ids // group_slots)[:, None]) & (
        own_rank[None, :] == (slot_ids % group_slots)[:, None]
    )
    picked = jnp.sum(jnp.where(hit, group_ids[None, :], 0), axis=1)
    send_pick = jnp.where(
        jnp.any(hit, axis=1)[:, None], picked[:, None] * SB + lane[None, :], local_len
    ).reshape(-1)
    hit_in = (dest_g[:, None, :] == my_index) & (
        rank_g[:, None, :] == jnp.arange(group_slots, dtype=jnp.int32)[None, :, None]
    )
    picked_in = jnp.sum(jnp.where(hit_in, group_ids[None, None, :], 0), axis=2)
    elem = (picked_in[:, :, None] * SB + lane[None, None, :]).reshape(groups, capacity)
    parent_of_slot = jnp.take_along_axis(src_map, elem, axis=1)
    parent_blk = parent_of_slot // block_width
    landing = parent_blk // groups * block_width + parent_of_slot % block_width
    valid = jnp.repeat(jnp.any(hit_in, axis=2), SB, axis=1)
    landing = jnp.where(valid, landing, parent_len).reshape(-1)
    match = landing[None, :] == jnp.arange(parent_len, dtype=jnp.int32)[:, None]
    recv_pick = jnp.where(
        jnp.any(match, axis=1), jnp.argmax(match, axis=1).astype(jnp.int32), groups * capacity
    )
    return (send_pick, recv_pick)


def factor_block(block_in, tile_size):
    order_len = block_in.shape[0]
    num_tiles = order_len // tile_size
    identity = jnp.eye(tile_size, dtype=jnp.float32)
    zero_tile = jnp.zeros((tile_size, tile_size), jnp.float32)
    low_tiles = [[zero_tile for col_tile in range(num_tiles)] for row_tile in range(num_tiles)]
    diag_inverses = []
    working = block_in
    for col_tile in range(num_tiles):
        tile_start = col_tile * tile_size
        tile_end = tile_start + tile_size
        diag_tile = jnp.linalg.cholesky(working[tile_start:tile_end, tile_start:tile_end])
        diag_inverse = jax.scipy.linalg.solve_triangular(diag_tile, identity, lower=True)
        low_tiles[col_tile][col_tile] = diag_tile
        diag_inverses.append(diag_inverse)
        if tile_end < order_len:
            stripe_rows = jnp.dot(
                working[tile_end:, tile_start:tile_end], diag_inverse.T, precision=HIGHEST
            )
            for row_tile in range(col_tile + 1, num_tiles):
                offset = (row_tile - col_tile - 1) * tile_size
                low_tiles[row_tile][col_tile] = stripe_rows[offset : offset + tile_size]
            working = working.at[tile_end:, tile_end:].add(
                -jnp.dot(stripe_rows, stripe_rows.T, precision=HIGHEST)
            )
    inv_tiles = [[zero_tile for col_tile in range(num_tiles)] for row_tile in range(num_tiles)]
    for row_tile in range(num_tiles):
        inv_tiles[row_tile][row_tile] = diag_inverses[row_tile]
        for col_tile in range(row_tile - 1, -1, -1):
            partial_sum = zero_tile
            for mid_tile in range(col_tile, row_tile):
                partial_sum = partial_sum + jnp.dot(
                    low_tiles[row_tile][mid_tile], inv_tiles[mid_tile][col_tile], precision=HIGHEST
                )
            inv_tiles[row_tile][col_tile] = -jnp.dot(
                diag_inverses[row_tile], partial_sum, precision=HIGHEST
            )
    return (jnp.block(low_tiles), jnp.block(inv_tiles))


def lower_inverse(low, tile):
    order = low.shape[0]
    count = order // tile
    diag = jnp.stack([low[k * tile : (k + 1) * tile, k * tile : (k + 1) * tile] for k in range(count)])
    eye = jnp.broadcast_to(jnp.eye(tile, dtype=low.dtype), diag.shape)
    inv = jax.scipy.linalg.solve_triangular(diag, eye, lower=True)
    size = tile
    while size < order:
        pairs = inv.shape[0] // 2
        upper = inv[0::2]
        lower = inv[1::2]
        off = jnp.stack(
            [
                low[(2 * p + 1) * size : (2 * p + 2) * size, 2 * p * size : (2 * p + 1) * size]
                for p in range(pairs)
            ]
        )
        mixed = -jnp.einsum(
            "pij,pjk->pik",
            jnp.einsum("pij,pjk->pik", lower, off, precision=HIGHEST),
            upper,
            precision=HIGHEST,
        )
        zero = jnp.zeros_like(upper)
        top = jnp.concatenate([upper, zero], axis=2)
        bottom = jnp.concatenate([mixed, lower], axis=2)
        inv = jnp.concatenate([top, bottom], axis=1)
        size *= 2
    return inv[0]


def local(front, child_block, child_to_parent):
    grid_rows = lax.axis_size("prow")
    grid_cols = lax.axis_size("pcol")
    my_row = lax.axis_index("prow")
    my_col = lax.axis_index("pcol")
    row_blocks = front.shape[0]
    block_width = front.shape[2]
    col_blocks = front.shape[3]
    child_rblocks = child_block.shape[0]
    child_cblocks = child_block.shape[3]
    local_rows = row_blocks * block_width
    local_cols = col_blocks * block_width
    child_rows = child_rblocks * block_width
    child_cols = child_cblocks * block_width
    cap_rows = 2 * child_rows // grid_rows
    cap_cols = 2 * child_cols // grid_cols
    tile_size = min(64, block_width)
    row_send, row_recv = route_tables(
        child_to_parent, child_rblocks, grid_rows, block_width, my_row, cap_rows, local_rows
    )
    col_send, col_recv = route_tables(
        child_to_parent, child_cblocks, grid_cols, block_width, my_col, cap_cols, local_cols
    )
    child_local = child_block.reshape(child_rows, child_cols)
    staged = jnp.take(jnp.pad(child_local, ((0, 0), (0, 1))), col_send, axis=1)
    staged = lax.all_to_all(
        staged.reshape(child_rows, grid_cols, cap_cols), "pcol", split_axis=1, concat_axis=1, tiled=True
    ).reshape(child_rows, grid_cols * cap_cols)
    moved = jnp.take(jnp.pad(staged, ((0, 1), (0, 0))), row_send, axis=0)
    moved = lax.all_to_all(
        moved.reshape(grid_rows, cap_rows, grid_cols * cap_cols), "prow", split_axis=0, concat_axis=0, tiled=True
    )
    arrived = jnp.pad(moved.reshape(grid_rows * cap_rows, grid_cols * cap_cols), ((0, 1), (0, 1)))
    added = jnp.take(jnp.take(arrived, row_recv, axis=0), col_recv, axis=1)
    matrix = front.reshape(local_rows, local_cols) + added
    panel = NP * block_width
    row_blk = jnp.repeat(jnp.arange(row_blocks, dtype=jnp.int32) * grid_rows + my_row, block_width)
    col_blk = jnp.repeat(jnp.arange(col_blocks, dtype=jnp.int32) * grid_cols + my_col, block_width)
    first_cols = matrix[:, :block_width]
    first_rows = matrix[:block_width, :]
    zero_cols = jnp.zeros_like(first_cols)
    zero_rows = jnp.zeros_like(first_rows)
    x_part = jnp.concatenate(
        [jnp.where(my_col == p, first_cols, zero_cols) for p in range(NP)], axis=1
    )
    y_part = jnp.concatenate(
        [jnp.where(my_row == p, first_rows, zero_rows) for p in range(NP)], axis=0
    )
    panel_ids = jnp.arange(panel, dtype=jnp.int32)
    child_row_ids = (
        (jnp.arange(child_rblocks, dtype=jnp.int32)[:, None] * grid_rows + my_row) * block_width
        + jnp.arange(block_width, dtype=jnp.int32)[None, :]
    ).reshape(-1)
    child_col_ids = (
        (jnp.arange(child_cblocks, dtype=jnp.int32)[:, None] * grid_cols + my_col) * block_width
        + jnp.arange(block_width, dtype=jnp.int32)[None, :]
    ).reshape(-1)
    row_hit = (child_to_parent[child_row_ids][None, :] == panel_ids[:, None]).astype(jnp.float32)
    col_hit = (child_to_parent[child_col_ids][None, :] == panel_ids[:, None]).astype(jnp.float32)
    corner_child = jnp.dot(
        jnp.dot(row_hit, child_local, precision=HIGHEST), col_hit.T, precision=HIGHEST
    )
    corner = front[0, 0, :, 0, 0, :]
    zero_corner = jnp.zeros_like(corner)
    d_part = corner_child + jnp.concatenate(
        [
            jnp.concatenate(
                [
                    jnp.where((my_row == p) & (my_col == q), corner, zero_corner)
                    for q in range(NP)
                ],
                axis=1,
            )
            for p in range(NP)
        ],
        axis=0,
    )
    d_full = lax.psum(d_part, ("prow", "pcol"))
    d_full, x_part, y_part = lax.optimization_barrier((d_full, x_part, y_part))
    x_full = lax.psum(x_part, "pcol")
    y_full = lax.psum(y_part, "prow")
    low = jnp.tril(jnp.linalg.cholesky(d_full))
    low_inv = lower_inverse(low, min(128, panel))
    rows_f = jnp.dot(x_full, low_inv.T, precision=HIGHEST)
    cols_f = lax.dot_general(
        y_full, low_inv, (((0,), (1,)), ((), ())), precision=HIGHEST
    )
    low_rows = lax.dynamic_slice_in_dim(low, jnp.minimum(my_row, NP - 1) * block_width, block_width, 0)
    head = jnp.where(my_row < NP, low_rows, rows_f[:block_width])
    rows_f = jnp.concatenate([head, rows_f[block_width:]], axis=0)
    lane = jnp.arange(panel, dtype=jnp.int32)[None, :]
    keep_row = (row_blk[:, None] >= NP) | (lane < (row_blk[:, None] * block_width))
    rows_u = jnp.where(keep_row, rows_f, 0.0)
    cols_u = jnp.where((col_blk >= NP)[:, None], cols_f, 0.0)
    matrix = matrix - jnp.dot(rows_u, cols_u.T, precision=HIGHEST)
    out_first = matrix[:, :block_width]
    for p in range(NP):
        out_first = jnp.where(
            my_col == p, rows_f[:, p * block_width : (p + 1) * block_width], out_first
        )
    matrix = jnp.concatenate([out_first, matrix[:, block_width:]], axis=1)
    return matrix.reshape(front.shape)


def solution(mesh):
    in_specs = (
        P(None, "prow", None, None, "pcol", None),
        P(None, "prow", None, None, "pcol", None),
        P(),
    )
    out_specs = P(None, "prow", None, None, "pcol", None)
    return jax.shard_map(local, mesh=mesh, in_specs=in_specs, out_specs=out_specs, check_vma=False)
```

```python
import jax
import jax.numpy as jnp
from jax import lax
from jax.sharding import PartitionSpec as P

NP = 2
SB = 32


HIGHEST = lax.Precision.HIGHEST


def from_root(x, axis, root):
    mine = lax.axis_index(axis) == root
    return lax.psum(jnp.where(mine, x, jnp.zeros_like(x)), axis)


def slot_ranks(destiny, groups):
    one_hot = (destiny[:, :, None] == jnp.arange(groups, dtype=jnp.int32)[None, None, :]).astype(
        jnp.int32
    )
    return jnp.sum(jnp.cumsum(one_hot, axis=1) * one_hot, axis=2) - 1


def by_source(values, blocks_local, groups, block_width):
    return jnp.transpose(values.reshape(blocks_local, groups, block_width), (1, 0, 2)).reshape(
        groups, blocks_local * block_width
    )


def route_tables(mapping, blocks_local, groups, block_width, my_index, capacity, parent_len):
    local_len = blocks_local * block_width
    num_groups = local_len // SB
    group_slots = capacity // SB
    src_map = by_source(mapping, blocks_local, groups, block_width)
    dest_g = (src_map[:, ::SB] // block_width) % groups
    rank_g = slot_ranks(dest_g, groups)
    group_ids = jnp.arange(num_groups, dtype=jnp.int32)
    lane = jnp.arange(SB, dtype=jnp.int32)
    own_dest = lax.dynamic_index_in_dim(dest_g, my_index, 0, keepdims=False)
    own_rank = lax.dynamic_index_in_dim(rank_g, my_index, 0, keepdims=False)
    slot_ids = jnp.arange(groups * group_slots, dtype=jnp.int32)
    hit = (own_dest[None, :] == (slot_ids // group_slots)[:, None]) & (
        own_rank[None, :] == (slot_ids % group_slots)[:, None]
    )
    picked = jnp.sum(jnp.where(hit, group_ids[None, :], 0), axis=1)
    send_pick = jnp.where(
        jnp.any(hit, axis=1)[:, None], picked[:, None] * SB + lane[None, :], local_len
    ).reshape(-1)
    hit_in = (dest_g[:, None, :] == my_index) & (
        rank_g[:, None, :] == jnp.arange(group_slots, dtype=jnp.int32)[None, :, None]
    )
    picked_in = jnp.sum(jnp.where(hit_in, group_ids[None, None, :], 0), axis=2)
    elem = (picked_in[:, :, None] * SB + lane[None, None, :]).reshape(groups, capacity)
    parent_of_slot = jnp.take_along_axis(src_map, elem, axis=1)
    parent_blk = parent_of_slot // block_width
    landing = parent_blk // groups * block_width + parent_of_slot % block_width
    valid = jnp.repeat(jnp.any(hit_in, axis=2), SB, axis=1)
    landing = jnp.where(valid, landing, parent_len).reshape(-1)
    match = landing[None, :] == jnp.arange(parent_len, dtype=jnp.int32)[:, None]
    recv_pick = jnp.where(
        jnp.any(match, axis=1), jnp.argmax(match, axis=1).astype(jnp.int32), groups * capacity
    )
    return (send_pick, recv_pick)


def factor_block(block_in, tile_size):
    order_len = block_in.shape[0]
    num_tiles = order_len // tile_size
    identity = jnp.eye(tile_size, dtype=jnp.float32)
    zero_tile = jnp.zeros((tile_size, tile_size), jnp.float32)
    low_tiles = [[zero_tile for col_tile in range(num_tiles)] for row_tile in range(num_tiles)]
    diag_inverses = []
    working = block_in
    for col_tile in range(num_tiles):
        tile_start = col_tile * tile_size
        tile_end = tile_start + tile_size
        diag_tile = jnp.linalg.cholesky(working[tile_start:tile_end, tile_start:tile_end])
        diag_inverse = jax.scipy.linalg.solve_triangular(diag_tile, identity, lower=True)
        low_tiles[col_tile][col_tile] = diag_tile
        diag_inverses.append(diag_inverse)
        if tile_end < order_len:
            stripe_rows = jnp.dot(
                working[tile_end:, tile_start:tile_end], diag_inverse.T, precision=HIGHEST
            )
            for row_tile in range(col_tile + 1, num_tiles):
                offset = (row_tile - col_tile - 1) * tile_size
                low_tiles[row_tile][col_tile] = stripe_rows[offset : offset + tile_size]
            working = working.at[tile_end:, tile_end:].add(
                -jnp.dot(stripe_rows, stripe_rows.T, precision=HIGHEST)
            )
    inv_tiles = [[zero_tile for col_tile in range(num_tiles)] for row_tile in range(num_tiles)]
    for row_tile in range(num_tiles):
        inv_tiles[row_tile][row_tile] = diag_inverses[row_tile]
        for col_tile in range(row_tile - 1, -1, -1):
            partial_sum = zero_tile
            for mid_tile in range(col_tile, row_tile):
                partial_sum = partial_sum + jnp.dot(
                    low_tiles[row_tile][mid_tile], inv_tiles[mid_tile][col_tile], precision=HIGHEST
                )
            inv_tiles[row_tile][col_tile] = -jnp.dot(
                diag_inverses[row_tile], partial_sum, precision=HIGHEST
            )
    return (jnp.block(low_tiles), jnp.block(inv_tiles))


def lower_inverse(low, tile):
    order = low.shape[0]
    count = order // tile
    diag = jnp.stack([low[k * tile : (k + 1) * tile, k * tile : (k + 1) * tile] for k in range(count)])
    eye = jnp.broadcast_to(jnp.eye(tile, dtype=low.dtype), diag.shape)
    inv = jax.scipy.linalg.solve_triangular(diag, eye, lower=True)
    size = tile
    while size < order:
        pairs = inv.shape[0] // 2
        upper = inv[0::2]
        lower = inv[1::2]
        off = jnp.stack(
            [
                low[(2 * p + 1) * size : (2 * p + 2) * size, 2 * p * size : (2 * p + 1) * size]
                for p in range(pairs)
            ]
        )
        mixed = -jnp.einsum(
            "pij,pjk->pik",
            jnp.einsum("pij,pjk->pik", lower, off, precision=HIGHEST),
            upper,
            precision=HIGHEST,
        )
        zero = jnp.zeros_like(upper)
        top = jnp.concatenate([upper, zero], axis=2)
        bottom = jnp.concatenate([mixed, lower], axis=2)
        inv = jnp.concatenate([top, bottom], axis=1)
        size *= 2
    return inv[0]


def corner_part(front, child_local, child_to_parent, my_row, my_col, grid_rows, grid_cols):
    block_width = front.shape[2]
    child_rblocks = child_local.shape[0] // block_width
    child_cblocks = child_local.shape[1] // block_width
    panel = NP * block_width
    panel_ids = jnp.arange(panel, dtype=jnp.int32)
    child_row_ids = (
        (jnp.arange(child_rblocks, dtype=jnp.int32)[:, None] * grid_rows + my_row) * block_width
        + jnp.arange(block_width, dtype=jnp.int32)[None, :]
    ).reshape(-1)
    child_col_ids = (
        (jnp.arange(child_cblocks, dtype=jnp.int32)[:, None] * grid_cols + my_col) * block_width
        + jnp.arange(block_width, dtype=jnp.int32)[None, :]
    ).reshape(-1)
    row_hit = (child_to_parent[child_row_ids][None, :] == panel_ids[:, None]).astype(jnp.float32)
    col_hit = (child_to_parent[child_col_ids][None, :] == panel_ids[:, None]).astype(jnp.float32)
    corner_child = jnp.dot(
        jnp.dot(row_hit, child_local, precision=HIGHEST), col_hit.T, precision=HIGHEST
    )
    corner = front[0, 0, :, 0, 0, :]
    zero_corner = jnp.zeros_like(corner)
    return corner_child + jnp.concatenate(
        [
            jnp.concatenate(
                [
                    jnp.where((my_row == p) & (my_col == q), corner, zero_corner)
                    for q in range(NP)
                ],
                axis=1,
            )
            for p in range(NP)
        ],
        axis=0,
    )


def local(front, child_block, child_to_parent):
    grid_rows = lax.axis_size("prow")
    grid_cols = lax.axis_size("pcol")
    my_row = lax.axis_index("prow")
    my_col = lax.axis_index("pcol")
    row_blocks = front.shape[0]
    block_width = front.shape[2]
    col_blocks = front.shape[3]
    child_rblocks = child_block.shape[0]
    child_cblocks = child_block.shape[3]
    local_rows = row_blocks * block_width
    local_cols = col_blocks * block_width
    child_rows = child_rblocks * block_width
    child_cols = child_cblocks * block_width
    cap_rows = 2 * child_rows // grid_rows
    cap_cols = 2 * child_cols // grid_cols
    tile_size = min(64, block_width)
    row_send, row_recv = route_tables(
        child_to_parent, child_rblocks, grid_rows, block_width, my_row, cap_rows, local_rows
    )
    col_send, col_recv = route_tables(
        child_to_parent, child_cblocks, grid_cols, block_width, my_col, cap_cols, local_cols
    )
    child_local = child_block.reshape(child_rows, child_cols)
    staged = jnp.take(jnp.pad(child_local, ((0, 0), (0, 1))), col_send, axis=1)
    staged = lax.all_to_all(
        staged.reshape(child_rows, grid_cols, cap_cols), "pcol", split_axis=1, concat_axis=1, tiled=True
    ).reshape(child_rows, grid_cols * cap_cols)
    front_mat = front.reshape(local_rows, local_cols)
    d_part = corner_part(front, child_local, child_to_parent, my_row, my_col, grid_rows, grid_cols)
    staged, d_part, front_mat = lax.optimization_barrier((staged, d_part, front_mat))
    moved = jnp.take(jnp.pad(staged, ((0, 1), (0, 0))), row_send, axis=0)
    moved = lax.all_to_all(
        moved.reshape(grid_rows, cap_rows, grid_cols * cap_cols), "prow", split_axis=0, concat_axis=0, tiled=True
    )
    arrived = jnp.pad(moved.reshape(grid_rows * cap_rows, grid_cols * cap_cols), ((0, 1), (0, 1)))
    added = jnp.take(jnp.take(arrived, row_recv, axis=0), col_recv, axis=1)
    matrix = front_mat + added
    panel = NP * block_width
    row_blk = jnp.repeat(jnp.arange(row_blocks, dtype=jnp.int32) * grid_rows + my_row, block_width)
    col_blk = jnp.repeat(jnp.arange(col_blocks, dtype=jnp.int32) * grid_cols + my_col, block_width)
    first_cols = matrix[:, :block_width]
    first_rows = matrix[:block_width, :]
    zero_cols = jnp.zeros_like(first_cols)
    zero_rows = jnp.zeros_like(first_rows)
    x_part = jnp.concatenate(
        [jnp.where(my_col == p, first_cols, zero_cols) for p in range(NP)], axis=1
    )
    y_part = jnp.concatenate(
        [jnp.where(my_row == p, first_rows, zero_rows) for p in range(NP)], axis=0
    )
    d_full = lax.psum(d_part, ("prow", "pcol"))
    d_full, x_part, y_part = lax.optimization_barrier((d_full, x_part, y_part))
    x_full = lax.psum(x_part, "pcol")
    y_full = lax.psum(y_part, "prow")
    low = jnp.tril(jnp.linalg.cholesky(d_full))
    low_inv = lower_inverse(low, min(128, panel))
    rows_f = jnp.dot(x_full, low_inv.T, precision=HIGHEST)
    cols_f = lax.dot_general(
        y_full, low_inv, (((0,), (1,)), ((), ())), precision=HIGHEST
    )
    low_rows = lax.dynamic_slice_in_dim(low, jnp.minimum(my_row, NP - 1) * block_width, block_width, 0)
    head = jnp.where(my_row < NP, low_rows, rows_f[:block_width])
    rows_f = jnp.concatenate([head, rows_f[block_width:]], axis=0)
    lane = jnp.arange(panel, dtype=jnp.int32)[None, :]
    keep_row = (row_blk[:, None] >= NP) | (lane < (row_blk[:, None] * block_width))
    rows_u = jnp.where(keep_row, rows_f, 0.0)
    cols_u = jnp.where((col_blk >= NP)[:, None], cols_f, 0.0)
    updated = matrix - jnp.dot(rows_u, cols_u.T, precision=HIGHEST)
    panel_src = jnp.where(my_col == 0, rows_f, jnp.roll(rows_f, -block_width, axis=1))
    out_lane = jnp.arange(local_cols, dtype=jnp.int32)[None, :]
    matrix = jnp.where((out_lane < block_width) & (my_col < NP), panel_src, updated)
    return matrix.reshape(front.shape)


def solution(mesh):
    in_specs = (
        P(None, "prow", None, None, "pcol", None),
        P(None, "prow", None, None, "pcol", None),
        P(),
    )
    out_specs = P(None, "prow", None, None, "pcol", None)
    return jax.shard_map(local, mesh=mesh, in_specs=in_specs, out_specs=out_specs, check_vma=False)
```

```python
import jax
import jax.numpy as jnp
from jax import lax
from jax.sharding import PartitionSpec as P

NP = 2
SB = 32


HIGHEST = lax.Precision.HIGHEST


def from_root(x, axis, root):
    mine = lax.axis_index(axis) == root
    return lax.psum(jnp.where(mine, x, jnp.zeros_like(x)), axis)


def slot_ranks(destiny, groups):
    one_hot = (destiny[:, :, None] == jnp.arange(groups, dtype=jnp.int32)[None, None, :]).astype(
        jnp.int32
    )
    return jnp.sum(jnp.cumsum(one_hot, axis=1) * one_hot, axis=2) - 1


def by_source(values, blocks_local, groups, block_width):
    return jnp.transpose(values.reshape(blocks_local, groups, block_width), (1, 0, 2)).reshape(
        groups, blocks_local * block_width
    )


def route_tables(mapping, blocks_local, groups, block_width, my_index, capacity, parent_len):
    local_len = blocks_local * block_width
    num_groups = local_len // SB
    group_slots = capacity // SB
    src_map = by_source(mapping, blocks_local, groups, block_width)
    dest_g = (src_map[:, ::SB] // block_width) % groups
    rank_g = slot_ranks(dest_g, groups)
    group_ids = jnp.arange(num_groups, dtype=jnp.int32)
    lane = jnp.arange(SB, dtype=jnp.int32)
    own_dest = lax.dynamic_index_in_dim(dest_g, my_index, 0, keepdims=False)
    own_rank = lax.dynamic_index_in_dim(rank_g, my_index, 0, keepdims=False)
    slot_ids = jnp.arange(groups * group_slots, dtype=jnp.int32)
    hit = (own_dest[None, :] == (slot_ids // group_slots)[:, None]) & (
        own_rank[None, :] == (slot_ids % group_slots)[:, None]
    )
    picked = jnp.sum(jnp.where(hit, group_ids[None, :], 0), axis=1)
    send_pick = jnp.where(
        jnp.any(hit, axis=1)[:, None], picked[:, None] * SB + lane[None, :], local_len
    ).reshape(-1)
    hit_in = (dest_g[:, None, :] == my_index) & (
        rank_g[:, None, :] == jnp.arange(group_slots, dtype=jnp.int32)[None, :, None]
    )
    picked_in = jnp.sum(jnp.where(hit_in, group_ids[None, None, :], 0), axis=2)
    elem = (picked_in[:, :, None] * SB + lane[None, None, :]).reshape(groups, capacity)
    parent_of_slot = jnp.take_along_axis(src_map, elem, axis=1)
    parent_blk = parent_of_slot // block_width
    landing = parent_blk // groups * block_width + parent_of_slot % block_width
    valid = jnp.repeat(jnp.any(hit_in, axis=2), SB, axis=1)
    landing = jnp.where(valid, landing, parent_len).reshape(-1)
    match = landing[None, :] == jnp.arange(parent_len, dtype=jnp.int32)[:, None]
    recv_pick = jnp.where(
        jnp.any(match, axis=1), jnp.argmax(match, axis=1).astype(jnp.int32), groups * capacity
    )
    return (send_pick, recv_pick)


def factor_block(block_in, tile_size):
    order_len = block_in.shape[0]
    num_tiles = order_len // tile_size
    identity = jnp.eye(tile_size, dtype=jnp.float32)
    zero_tile = jnp.zeros((tile_size, tile_size), jnp.float32)
    low_tiles = [[zero_tile for col_tile in range(num_tiles)] for row_tile in range(num_tiles)]
    diag_inverses = []
    working = block_in
    for col_tile in range(num_tiles):
        tile_start = col_tile * tile_size
        tile_end = tile_start + tile_size
        diag_tile = jnp.linalg.cholesky(working[tile_start:tile_end, tile_start:tile_end])
        diag_inverse = jax.scipy.linalg.solve_triangular(diag_tile, identity, lower=True)
        low_tiles[col_tile][col_tile] = diag_tile
        diag_inverses.append(diag_inverse)
        if tile_end < order_len:
            stripe_rows = jnp.dot(
                working[tile_end:, tile_start:tile_end], diag_inverse.T, precision=HIGHEST
            )
            for row_tile in range(col_tile + 1, num_tiles):
                offset = (row_tile - col_tile - 1) * tile_size
                low_tiles[row_tile][col_tile] = stripe_rows[offset : offset + tile_size]
            working = working.at[tile_end:, tile_end:].add(
                -jnp.dot(stripe_rows, stripe_rows.T, precision=HIGHEST)
            )
    inv_tiles = [[zero_tile for col_tile in range(num_tiles)] for row_tile in range(num_tiles)]
    for row_tile in range(num_tiles):
        inv_tiles[row_tile][row_tile] = diag_inverses[row_tile]
        for col_tile in range(row_tile - 1, -1, -1):
            partial_sum = zero_tile
            for mid_tile in range(col_tile, row_tile):
                partial_sum = partial_sum + jnp.dot(
                    low_tiles[row_tile][mid_tile], inv_tiles[mid_tile][col_tile], precision=HIGHEST
                )
            inv_tiles[row_tile][col_tile] = -jnp.dot(
                diag_inverses[row_tile], partial_sum, precision=HIGHEST
            )
    return (jnp.block(low_tiles), jnp.block(inv_tiles))


def lower_inverse(low, tile):
    order = low.shape[0]
    count = order // tile
    diag = jnp.stack([low[k * tile : (k + 1) * tile, k * tile : (k + 1) * tile] for k in range(count)])
    eye = jnp.broadcast_to(jnp.eye(tile, dtype=low.dtype), diag.shape)
    inv = jax.scipy.linalg.solve_triangular(diag, eye, lower=True)
    size = tile
    while size < order:
        pairs = inv.shape[0] // 2
        upper = inv[0::2]
        lower = inv[1::2]
        off = jnp.stack(
            [
                low[(2 * p + 1) * size : (2 * p + 2) * size, 2 * p * size : (2 * p + 1) * size]
                for p in range(pairs)
            ]
        )
        mixed = -jnp.einsum(
            "pij,pjk->pik",
            jnp.einsum("pij,pjk->pik", lower, off, precision=HIGHEST),
            upper,
            precision=HIGHEST,
        )
        zero = jnp.zeros_like(upper)
        top = jnp.concatenate([upper, zero], axis=2)
        bottom = jnp.concatenate([mixed, lower], axis=2)
        inv = jnp.concatenate([top, bottom], axis=1)
        size *= 2
    return inv[0]


def corner_part(front, child_local, child_to_parent, my_row, my_col, grid_rows, grid_cols):
    block_width = front.shape[2]
    child_rblocks = child_local.shape[0] // block_width
    child_cblocks = child_local.shape[1] // block_width
    panel = NP * block_width
    panel_ids = jnp.arange(panel, dtype=jnp.int32)
    child_row_ids = (
        (jnp.arange(child_rblocks, dtype=jnp.int32)[:, None] * grid_rows + my_row) * block_width
        + jnp.arange(block_width, dtype=jnp.int32)[None, :]
    ).reshape(-1)
    child_col_ids = (
        (jnp.arange(child_cblocks, dtype=jnp.int32)[:, None] * grid_cols + my_col) * block_width
        + jnp.arange(block_width, dtype=jnp.int32)[None, :]
    ).reshape(-1)
    row_hit = (child_to_parent[child_row_ids][None, :] == panel_ids[:, None]).astype(jnp.float32)
    col_hit = (child_to_parent[child_col_ids][None, :] == panel_ids[:, None]).astype(jnp.float32)
    corner_child = jnp.dot(
        jnp.dot(row_hit, child_local, precision=HIGHEST), col_hit.T, precision=HIGHEST
    )
    corner = front[0, 0, :, 0, 0, :]
    zero_corner = jnp.zeros_like(corner)
    return corner_child + jnp.concatenate(
        [
            jnp.concatenate(
                [
                    jnp.where((my_row == p) & (my_col == q), corner, zero_corner)
                    for q in range(NP)
                ],
                axis=1,
            )
            for p in range(NP)
        ],
        axis=0,
    )


def local(front, child_block, child_to_parent):
    grid_rows = lax.axis_size("prow")
    grid_cols = lax.axis_size("pcol")
    my_row = lax.axis_index("prow")
    my_col = lax.axis_index("pcol")
    row_blocks = front.shape[0]
    block_width = front.shape[2]
    col_blocks = front.shape[3]
    child_rblocks = child_block.shape[0]
    child_cblocks = child_block.shape[3]
    local_rows = row_blocks * block_width
    local_cols = col_blocks * block_width
    child_rows = child_rblocks * block_width
    child_cols = child_cblocks * block_width
    cap_rows = 2 * child_rows // grid_rows
    cap_cols = 2 * child_cols // grid_cols
    tile_size = min(64, block_width)
    row_send, row_recv = route_tables(
        child_to_parent, child_rblocks, grid_rows, block_width, my_row, cap_rows, local_rows
    )
    col_send, col_recv = route_tables(
        child_to_parent, child_cblocks, grid_cols, block_width, my_col, cap_cols, local_cols
    )
    child_local = child_block.reshape(child_rows, child_cols)
    staged = jnp.take(jnp.pad(child_local, ((0, 0), (0, 1))), col_send, axis=1)
    d_part = corner_part(front, child_local, child_to_parent, my_row, my_col, grid_rows, grid_cols)
    staged, d_part = lax.optimization_barrier((staged, d_part))
    d_full = lax.psum(d_part, ("prow", "pcol"))
    staged = lax.all_to_all(
        staged.reshape(child_rows, grid_cols, cap_cols), "pcol", split_axis=1, concat_axis=1, tiled=True
    ).reshape(child_rows, grid_cols * cap_cols)
    front_mat = front.reshape(local_rows, local_cols)
    staged, front_mat = lax.optimization_barrier((staged, front_mat))
    moved = jnp.take(jnp.pad(staged, ((0, 1), (0, 0))), row_send, axis=0)
    moved = lax.all_to_all(
        moved.reshape(grid_rows, cap_rows, grid_cols * cap_cols), "prow", split_axis=0, concat_axis=0, tiled=True
    )
    arrived = jnp.pad(moved.reshape(grid_rows * cap_rows, grid_cols * cap_cols), ((0, 1), (0, 1)))
    added = jnp.take(jnp.take(arrived, row_recv, axis=0), col_recv, axis=1)
    matrix = front_mat + added
    panel = NP * block_width
    row_blk = jnp.repeat(jnp.arange(row_blocks, dtype=jnp.int32) * grid_rows + my_row, block_width)
    col_blk = jnp.repeat(jnp.arange(col_blocks, dtype=jnp.int32) * grid_cols + my_col, block_width)
    first_cols = matrix[:, :block_width]
    first_rows = matrix[:block_width, :]
    zero_cols = jnp.zeros_like(first_cols)
    zero_rows = jnp.zeros_like(first_rows)
    x_part = jnp.concatenate(
        [jnp.where(my_col == p, first_cols, zero_cols) for p in range(NP)], axis=1
    )
    y_part = jnp.concatenate(
        [jnp.where(my_row == p, first_rows, zero_rows) for p in range(NP)], axis=0
    )
    tile = min(128, block_width)
    low00 = jnp.tril(jnp.linalg.cholesky(d_full[:block_width, :block_width]))
    inv00 = lower_inverse(low00, tile)
    low00, inv00, d_full, x_part, y_part = lax.optimization_barrier((low00, inv00, d_full, x_part, y_part))
    x_full = lax.psum(x_part, "pcol")
    y_full = lax.psum(y_part, "prow")
    low10 = jnp.dot(d_full[block_width:panel, :block_width], inv00.T, precision=HIGHEST)
    schur = d_full[block_width:panel, block_width:panel] - jnp.dot(low10, low10.T, precision=HIGHEST)
    low11 = jnp.tril(jnp.linalg.cholesky(schur))
    inv11 = lower_inverse(low11, tile)
    inv10 = -jnp.dot(jnp.dot(inv11, low10, precision=HIGHEST), inv00, precision=HIGHEST)
    zero_blk = jnp.zeros_like(low00)
    low = jnp.concatenate(
        [jnp.concatenate([low00, zero_blk], axis=1), jnp.concatenate([low10, low11], axis=1)], axis=0
    )
    low_inv = jnp.concatenate(
        [jnp.concatenate([inv00, zero_blk], axis=1), jnp.concatenate([inv10, inv11], axis=1)], axis=0
    )
    rows_f = jnp.dot(x_full, low_inv.T, precision=HIGHEST)
    cols_f = lax.dot_general(
        y_full, low_inv, (((0,), (1,)), ((), ())), precision=HIGHEST
    )
    low_rows = lax.dynamic_slice_in_dim(low, jnp.minimum(my_row, NP - 1) * block_width, block_width, 0)
    head = jnp.where(my_row < NP, low_rows, rows_f[:block_width])
    rows_f = jnp.concatenate([head, rows_f[block_width:]], axis=0)
    lane = jnp.arange(panel, dtype=jnp.int32)[None, :]
    keep_row = (row_blk[:, None] >= NP) | (lane < (row_blk[:, None] * block_width))
    rows_u = jnp.where(keep_row, rows_f, 0.0)
    cols_u = jnp.where((col_blk >= NP)[:, None], cols_f, 0.0)
    updated = matrix - jnp.dot(rows_u, cols_u.T, precision=HIGHEST)
    panel_src = jnp.where(my_col == 0, rows_f, jnp.roll(rows_f, -block_width, axis=1))
    out_lane = jnp.arange(local_cols, dtype=jnp.int32)[None, :]
    matrix = jnp.where((out_lane < block_width) & (my_col < NP), panel_src, updated)
    return matrix.reshape(front.shape)


def solution(mesh):
    in_specs = (
        P(None, "prow", None, None, "pcol", None),
        P(None, "prow", None, None, "pcol", None),
        P(),
    )
    out_specs = P(None, "prow", None, None, "pcol", None)
    return jax.shard_map(local, mesh=mesh, in_specs=in_specs, out_specs=out_specs, check_vma=False)
```

```python
import jax
import jax.numpy as jnp
from jax import lax
from jax.sharding import PartitionSpec as P

NP = 2
SB = 32


HIGHEST = lax.Precision.HIGHEST


def from_root(x, axis, root):
    mine = lax.axis_index(axis) == root
    return lax.psum(jnp.where(mine, x, jnp.zeros_like(x)), axis)


def slot_ranks(destiny, groups):
    one_hot = (destiny[:, :, None] == jnp.arange(groups, dtype=jnp.int32)[None, None, :]).astype(
        jnp.int32
    )
    return jnp.sum(jnp.cumsum(one_hot, axis=1) * one_hot, axis=2) - 1


def by_source(values, blocks_local, groups, block_width):
    return jnp.transpose(values.reshape(blocks_local, groups, block_width), (1, 0, 2)).reshape(
        groups, blocks_local * block_width
    )


def route_tables(mapping, blocks_local, groups, block_width, my_index, capacity, parent_len):
    local_len = blocks_local * block_width
    num_groups = local_len // SB
    group_slots = capacity // SB
    src_map = by_source(mapping, blocks_local, groups, block_width)
    dest_g = (src_map[:, ::SB] // block_width) % groups
    rank_g = slot_ranks(dest_g, groups)
    group_ids = jnp.arange(num_groups, dtype=jnp.int32)
    lane = jnp.arange(SB, dtype=jnp.int32)
    own_dest = lax.dynamic_index_in_dim(dest_g, my_index, 0, keepdims=False)
    own_rank = lax.dynamic_index_in_dim(rank_g, my_index, 0, keepdims=False)
    slot_ids = jnp.arange(groups * group_slots, dtype=jnp.int32)
    hit = (own_dest[None, :] == (slot_ids // group_slots)[:, None]) & (
        own_rank[None, :] == (slot_ids % group_slots)[:, None]
    )
    picked = jnp.sum(jnp.where(hit, group_ids[None, :], 0), axis=1)
    send_pick = jnp.where(
        jnp.any(hit, axis=1)[:, None], picked[:, None] * SB + lane[None, :], local_len
    ).reshape(-1)
    hit_in = (dest_g[:, None, :] == my_index) & (
        rank_g[:, None, :] == jnp.arange(group_slots, dtype=jnp.int32)[None, :, None]
    )
    picked_in = jnp.sum(jnp.where(hit_in, group_ids[None, None, :], 0), axis=2)
    elem = (picked_in[:, :, None] * SB + lane[None, None, :]).reshape(groups, capacity)
    parent_of_slot = jnp.take_along_axis(src_map, elem, axis=1)
    parent_blk = parent_of_slot // block_width
    landing = parent_blk // groups * block_width + parent_of_slot % block_width
    valid = jnp.repeat(jnp.any(hit_in, axis=2), SB, axis=1)
    landing = jnp.where(valid, landing, parent_len).reshape(-1)
    match = landing[None, :] == jnp.arange(parent_len, dtype=jnp.int32)[:, None]
    recv_pick = jnp.where(
        jnp.any(match, axis=1), jnp.argmax(match, axis=1).astype(jnp.int32), groups * capacity
    )
    return (send_pick, recv_pick)


def factor_block(block_in, tile_size):
    order_len = block_in.shape[0]
    num_tiles = order_len // tile_size
    identity = jnp.eye(tile_size, dtype=jnp.float32)
    zero_tile = jnp.zeros((tile_size, tile_size), jnp.float32)
    low_tiles = [[zero_tile for col_tile in range(num_tiles)] for row_tile in range(num_tiles)]
    diag_inverses = []
    working = block_in
    for col_tile in range(num_tiles):
        tile_start = col_tile * tile_size
        tile_end = tile_start + tile_size
        diag_tile = jnp.linalg.cholesky(working[tile_start:tile_end, tile_start:tile_end])
        diag_inverse = jax.scipy.linalg.solve_triangular(diag_tile, identity, lower=True)
        low_tiles[col_tile][col_tile] = diag_tile
        diag_inverses.append(diag_inverse)
        if tile_end < order_len:
            stripe_rows = jnp.dot(
                working[tile_end:, tile_start:tile_end], diag_inverse.T, precision=HIGHEST
            )
            for row_tile in range(col_tile + 1, num_tiles):
                offset = (row_tile - col_tile - 1) * tile_size
                low_tiles[row_tile][col_tile] = stripe_rows[offset : offset + tile_size]
            working = working.at[tile_end:, tile_end:].add(
                -jnp.dot(stripe_rows, stripe_rows.T, precision=HIGHEST)
            )
    inv_tiles = [[zero_tile for col_tile in range(num_tiles)] for row_tile in range(num_tiles)]
    for row_tile in range(num_tiles):
        inv_tiles[row_tile][row_tile] = diag_inverses[row_tile]
        for col_tile in range(row_tile - 1, -1, -1):
            partial_sum = zero_tile
            for mid_tile in range(col_tile, row_tile):
                partial_sum = partial_sum + jnp.dot(
                    low_tiles[row_tile][mid_tile], inv_tiles[mid_tile][col_tile], precision=HIGHEST
                )
            inv_tiles[row_tile][col_tile] = -jnp.dot(
                diag_inverses[row_tile], partial_sum, precision=HIGHEST
            )
    return (jnp.block(low_tiles), jnp.block(inv_tiles))


def lower_inverse(low, tile):
    order = low.shape[0]
    count = order // tile
    diag = jnp.stack([low[k * tile : (k + 1) * tile, k * tile : (k + 1) * tile] for k in range(count)])
    eye = jnp.broadcast_to(jnp.eye(tile, dtype=low.dtype), diag.shape)
    inv = jax.scipy.linalg.solve_triangular(diag, eye, lower=True)
    size = tile
    while size < order:
        pairs = inv.shape[0] // 2
        upper = inv[0::2]
        lower = inv[1::2]
        off = jnp.stack(
            [
                low[(2 * p + 1) * size : (2 * p + 2) * size, 2 * p * size : (2 * p + 1) * size]
                for p in range(pairs)
            ]
        )
        mixed = -jnp.einsum(
            "pij,pjk->pik",
            jnp.einsum("pij,pjk->pik", lower, off, precision=HIGHEST),
            upper,
            precision=HIGHEST,
        )
        zero = jnp.zeros_like(upper)
        top = jnp.concatenate([upper, zero], axis=2)
        bottom = jnp.concatenate([mixed, lower], axis=2)
        inv = jnp.concatenate([top, bottom], axis=1)
        size *= 2
    return inv[0]


def corner_part(front, child_local, child_to_parent, my_row, my_col, grid_rows, grid_cols):
    block_width = front.shape[2]
    child_rblocks = child_local.shape[0] // block_width
    child_cblocks = child_local.shape[1] // block_width
    panel = NP * block_width
    panel_ids = jnp.arange(panel, dtype=jnp.int32)
    child_row_ids = (
        (jnp.arange(child_rblocks, dtype=jnp.int32)[:, None] * grid_rows + my_row) * block_width
        + jnp.arange(block_width, dtype=jnp.int32)[None, :]
    ).reshape(-1)
    child_col_ids = (
        (jnp.arange(child_cblocks, dtype=jnp.int32)[:, None] * grid_cols + my_col) * block_width
        + jnp.arange(block_width, dtype=jnp.int32)[None, :]
    ).reshape(-1)
    row_hit = (child_to_parent[child_row_ids][None, :] == panel_ids[:, None]).astype(jnp.float32)
    col_hit = (child_to_parent[child_col_ids][None, :] == panel_ids[:, None]).astype(jnp.float32)
    corner_child = jnp.dot(
        jnp.dot(row_hit, child_local, precision=HIGHEST), col_hit.T, precision=HIGHEST
    )
    corner = front[0, 0, :, 0, 0, :]
    zero_corner = jnp.zeros_like(corner)
    return corner_child + jnp.concatenate(
        [
            jnp.concatenate(
                [
                    jnp.where((my_row == p) & (my_col == q), corner, zero_corner)
                    for q in range(NP)
                ],
                axis=1,
            )
            for p in range(NP)
        ],
        axis=0,
    )


def local(front, child_block, child_to_parent):
    grid_rows = lax.axis_size("prow")
    grid_cols = lax.axis_size("pcol")
    my_row = lax.axis_index("prow")
    my_col = lax.axis_index("pcol")
    row_blocks = front.shape[0]
    block_width = front.shape[2]
    col_blocks = front.shape[3]
    child_rblocks = child_block.shape[0]
    child_cblocks = child_block.shape[3]
    local_rows = row_blocks * block_width
    local_cols = col_blocks * block_width
    child_rows = child_rblocks * block_width
    child_cols = child_cblocks * block_width
    cap_rows = 2 * child_rows // grid_rows
    cap_cols = 2 * child_cols // grid_cols
    tile_size = min(64, block_width)
    row_send, row_recv = route_tables(
        child_to_parent, child_rblocks, grid_rows, block_width, my_row, cap_rows, local_rows
    )
    col_send, col_recv = route_tables(
        child_to_parent, child_cblocks, grid_cols, block_width, my_col, cap_cols, local_cols
    )
    child_local = child_block.reshape(child_rows, child_cols)
    d_part = corner_part(front, child_local, child_to_parent, my_row, my_col, grid_rows, grid_cols)
    d_full = lax.psum(d_part, ("prow", "pcol"))
    staged = jnp.take(jnp.pad(child_local, ((0, 0), (0, 1))), col_send, axis=1)
    staged = lax.all_to_all(
        staged.reshape(child_rows, grid_cols, cap_cols), "pcol", split_axis=1, concat_axis=1, tiled=True
    ).reshape(child_rows, grid_cols * cap_cols)
    front_mat = front.reshape(local_rows, local_cols)
    staged, front_mat = lax.optimization_barrier((staged, front_mat))
    moved = jnp.take(jnp.pad(staged, ((0, 1), (0, 0))), row_send, axis=0)
    moved = lax.all_to_all(
        moved.reshape(grid_rows, cap_rows, grid_cols * cap_cols), "prow", split_axis=0, concat_axis=0, tiled=True
    )
    arrived = jnp.pad(moved.reshape(grid_rows * cap_rows, grid_cols * cap_cols), ((0, 1), (0, 1)))
    added = jnp.take(jnp.take(arrived, row_recv, axis=0), col_recv, axis=1)
    matrix = front_mat + added
    panel = NP * block_width
    row_blk = jnp.repeat(jnp.arange(row_blocks, dtype=jnp.int32) * grid_rows + my_row, block_width)
    col_blk = jnp.repeat(jnp.arange(col_blocks, dtype=jnp.int32) * grid_cols + my_col, block_width)
    first_cols = matrix[:, :block_width]
    first_rows = matrix[:block_width, :]
    zero_cols = jnp.zeros_like(first_cols)
    zero_rows = jnp.zeros_like(first_rows)
    x_part = jnp.concatenate(
        [jnp.where(my_col == p, first_cols, zero_cols) for p in range(NP)], axis=1
    )
    y_part = jnp.concatenate(
        [jnp.where(my_row == p, first_rows, zero_rows) for p in range(NP)], axis=0
    )
    d_full, x_part, y_part = lax.optimization_barrier((d_full, x_part, y_part))
    x_full = lax.psum(x_part, "pcol")
    y_full = lax.psum(y_part, "prow")
    low = jnp.tril(jnp.linalg.cholesky(d_full))
    low_inv = lower_inverse(low, min(128, panel))
    rows_f = jnp.dot(x_full, low_inv.T, precision=HIGHEST)
    cols_f = lax.dot_general(
        y_full, low_inv, (((0,), (1,)), ((), ())), precision=HIGHEST
    )
    low_rows = lax.dynamic_slice_in_dim(low, jnp.minimum(my_row, NP - 1) * block_width, block_width, 0)
    head = jnp.where(my_row < NP, low_rows, rows_f[:block_width])
    rows_f = jnp.concatenate([head, rows_f[block_width:]], axis=0)
    lane = jnp.arange(panel, dtype=jnp.int32)[None, :]
    keep_row = (row_blk[:, None] >= NP) | (lane < (row_blk[:, None] * block_width))
    rows_u = jnp.where(keep_row, rows_f, 0.0)
    cols_u = jnp.where((col_blk >= NP)[:, None], cols_f, 0.0)
    updated = matrix - jnp.dot(rows_u, cols_u.T, precision=HIGHEST)
    panel_src = jnp.where(my_col == 0, rows_f, jnp.roll(rows_f, -block_width, axis=1))
    out_lane = jnp.arange(local_cols, dtype=jnp.int32)[None, :]
    matrix = jnp.where((out_lane < block_width) & (my_col < NP), panel_src, updated)
    return matrix.reshape(front.shape)


def solution(mesh):
    in_specs = (
        P(None, "prow", None, None, "pcol", None),
        P(None, "prow", None, None, "pcol", None),
        P(),
    )
    out_specs = P(None, "prow", None, None, "pcol", None)
    return jax.shard_map(local, mesh=mesh, in_specs=in_specs, out_specs=out_specs, check_vma=False)
```

```python
import jax
import jax.numpy as jnp
from jax import lax
from jax.sharding import PartitionSpec as P

NP = 2
SB = 32


HIGHEST = lax.Precision.HIGHEST


def from_root(x, axis, root):
    mine = lax.axis_index(axis) == root
    return lax.psum(jnp.where(mine, x, jnp.zeros_like(x)), axis)


def slot_ranks(destiny, groups):
    one_hot = (destiny[:, :, None] == jnp.arange(groups, dtype=jnp.int32)[None, None, :]).astype(
        jnp.int32
    )
    return jnp.sum(jnp.cumsum(one_hot, axis=1) * one_hot, axis=2) - 1


def by_source(values, blocks_local, groups, block_width):
    return jnp.transpose(values.reshape(blocks_local, groups, block_width), (1, 0, 2)).reshape(
        groups, blocks_local * block_width
    )


def route_tables(mapping, blocks_local, groups, block_width, my_index, capacity, parent_len):
    local_len = blocks_local * block_width
    num_groups = local_len // SB
    group_slots = capacity // SB
    src_map = by_source(mapping, blocks_local, groups, block_width)
    dest_g = (src_map[:, ::SB] // block_width) % groups
    rank_g = slot_ranks(dest_g, groups)
    group_ids = jnp.arange(num_groups, dtype=jnp.int32)
    lane = jnp.arange(SB, dtype=jnp.int32)
    own_dest = lax.dynamic_index_in_dim(dest_g, my_index, 0, keepdims=False)
    own_rank = lax.dynamic_index_in_dim(rank_g, my_index, 0, keepdims=False)
    slot_ids = jnp.arange(groups * group_slots, dtype=jnp.int32)
    hit = (own_dest[None, :] == (slot_ids // group_slots)[:, None]) & (
        own_rank[None, :] == (slot_ids % group_slots)[:, None]
    )
    picked = jnp.sum(jnp.where(hit, group_ids[None, :], 0), axis=1)
    send_pick = jnp.where(
        jnp.any(hit, axis=1)[:, None], picked[:, None] * SB + lane[None, :], local_len
    ).reshape(-1)
    hit_in = (dest_g[:, None, :] == my_index) & (
        rank_g[:, None, :] == jnp.arange(group_slots, dtype=jnp.int32)[None, :, None]
    )
    picked_in = jnp.sum(jnp.where(hit_in, group_ids[None, None, :], 0), axis=2)
    elem = (picked_in[:, :, None] * SB + lane[None, None, :]).reshape(groups, capacity)
    parent_of_slot = jnp.take_along_axis(src_map, elem, axis=1)
    parent_blk = parent_of_slot // block_width
    landing = parent_blk // groups * block_width + parent_of_slot % block_width
    valid = jnp.repeat(jnp.any(hit_in, axis=2), SB, axis=1)
    landing = jnp.where(valid, landing, parent_len).reshape(-1)
    match = landing[None, :] == jnp.arange(parent_len, dtype=jnp.int32)[:, None]
    recv_pick = jnp.where(
        jnp.any(match, axis=1), jnp.argmax(match, axis=1).astype(jnp.int32), groups * capacity
    )
    return (send_pick, recv_pick)


def factor_block(block_in, tile_size):
    order_len = block_in.shape[0]
    num_tiles = order_len // tile_size
    identity = jnp.eye(tile_size, dtype=jnp.float32)
    zero_tile = jnp.zeros((tile_size, tile_size), jnp.float32)
    low_tiles = [[zero_tile for col_tile in range(num_tiles)] for row_tile in range(num_tiles)]
    diag_inverses = []
    working = block_in
    for col_tile in range(num_tiles):
        tile_start = col_tile * tile_size
        tile_end = tile_start + tile_size
        diag_tile = jnp.linalg.cholesky(working[tile_start:tile_end, tile_start:tile_end])
        diag_inverse = jax.scipy.linalg.solve_triangular(diag_tile, identity, lower=True)
        low_tiles[col_tile][col_tile] = diag_tile
        diag_inverses.append(diag_inverse)
        if tile_end < order_len:
            stripe_rows = jnp.dot(
                working[tile_end:, tile_start:tile_end], diag_inverse.T, precision=HIGHEST
            )
            for row_tile in range(col_tile + 1, num_tiles):
                offset = (row_tile - col_tile - 1) * tile_size
                low_tiles[row_tile][col_tile] = stripe_rows[offset : offset + tile_size]
            working = working.at[tile_end:, tile_end:].add(
                -jnp.dot(stripe_rows, stripe_rows.T, precision=HIGHEST)
            )
    inv_tiles = [[zero_tile for col_tile in range(num_tiles)] for row_tile in range(num_tiles)]
    for row_tile in range(num_tiles):
        inv_tiles[row_tile][row_tile] = diag_inverses[row_tile]
        for col_tile in range(row_tile - 1, -1, -1):
            partial_sum = zero_tile
            for mid_tile in range(col_tile, row_tile):
                partial_sum = partial_sum + jnp.dot(
                    low_tiles[row_tile][mid_tile], inv_tiles[mid_tile][col_tile], precision=HIGHEST
                )
            inv_tiles[row_tile][col_tile] = -jnp.dot(
                diag_inverses[row_tile], partial_sum, precision=HIGHEST
            )
    return (jnp.block(low_tiles), jnp.block(inv_tiles))


def lower_inverse(low, tile):
    order = low.shape[0]
    count = order // tile
    diag = jnp.stack([low[k * tile : (k + 1) * tile, k * tile : (k + 1) * tile] for k in range(count)])
    eye = jnp.broadcast_to(jnp.eye(tile, dtype=low.dtype), diag.shape)
    inv = jax.scipy.linalg.solve_triangular(diag, eye, lower=True)
    size = tile
    while size < order:
        pairs = inv.shape[0] // 2
        upper = inv[0::2]
        lower = inv[1::2]
        off = jnp.stack(
            [
                low[(2 * p + 1) * size : (2 * p + 2) * size, 2 * p * size : (2 * p + 1) * size]
                for p in range(pairs)
            ]
        )
        mixed = -jnp.einsum(
            "pij,pjk->pik",
            jnp.einsum("pij,pjk->pik", lower, off, precision=HIGHEST),
            upper,
            precision=HIGHEST,
        )
        zero = jnp.zeros_like(upper)
        top = jnp.concatenate([upper, zero], axis=2)
        bottom = jnp.concatenate([mixed, lower], axis=2)
        inv = jnp.concatenate([top, bottom], axis=1)
        size *= 2
    return inv[0]


def corner_part(front, child_local, child_to_parent, my_row, my_col, grid_rows, grid_cols):
    block_width = front.shape[2]
    child_rblocks = child_local.shape[0] // block_width
    child_cblocks = child_local.shape[1] // block_width
    panel = NP * block_width
    panel_ids = jnp.arange(panel, dtype=jnp.int32)
    child_row_ids = (
        (jnp.arange(child_rblocks, dtype=jnp.int32)[:, None] * grid_rows + my_row) * block_width
        + jnp.arange(block_width, dtype=jnp.int32)[None, :]
    ).reshape(-1)
    child_col_ids = (
        (jnp.arange(child_cblocks, dtype=jnp.int32)[:, None] * grid_cols + my_col) * block_width
        + jnp.arange(block_width, dtype=jnp.int32)[None, :]
    ).reshape(-1)
    row_hit = (child_to_parent[child_row_ids][None, :] == panel_ids[:, None]).astype(jnp.float32)
    col_hit = (child_to_parent[child_col_ids][None, :] == panel_ids[:, None]).astype(jnp.float32)
    corner_child = jnp.dot(
        jnp.dot(row_hit, child_local, precision=HIGHEST), col_hit.T, precision=HIGHEST
    )
    corner = front[0, 0, :, 0, 0, :]
    zero_corner = jnp.zeros_like(corner)
    return corner_child + jnp.concatenate(
        [
            jnp.concatenate(
                [
                    jnp.where((my_row == p) & (my_col == q), corner, zero_corner)
                    for q in range(NP)
                ],
                axis=1,
            )
            for p in range(NP)
        ],
        axis=0,
    )


def local(front, child_block, child_to_parent):
    grid_rows = lax.axis_size("prow")
    grid_cols = lax.axis_size("pcol")
    my_row = lax.axis_index("prow")
    my_col = lax.axis_index("pcol")
    row_blocks = front.shape[0]
    block_width = front.shape[2]
    col_blocks = front.shape[3]
    child_rblocks = child_block.shape[0]
    child_cblocks = child_block.shape[3]
    local_rows = row_blocks * block_width
    local_cols = col_blocks * block_width
    child_rows = child_rblocks * block_width
    child_cols = child_cblocks * block_width
    cap_rows = 2 * child_rows // grid_rows
    cap_cols = 2 * child_cols // grid_cols
    tile_size = min(64, block_width)
    row_send, row_recv = route_tables(
        child_to_parent, child_rblocks, grid_rows, block_width, my_row, cap_rows, local_rows
    )
    col_send, col_recv = route_tables(
        child_to_parent, child_cblocks, grid_cols, block_width, my_col, cap_cols, local_cols
    )
    child_local = child_block.reshape(child_rows, child_cols)
    d_part = corner_part(front, child_local, child_to_parent, my_row, my_col, grid_rows, grid_cols)
    half = d_part.shape[0] // 2
    d_low = lax.psum(
        jnp.concatenate([d_part[:half, :half], d_part[half:, :half], d_part[half:, half:]], axis=0),
        ("prow", "pcol"),
    )
    d_full = jnp.concatenate(
        [
            jnp.concatenate([d_low[:half], d_low[half : 2 * half].T], axis=1),
            jnp.concatenate([d_low[half : 2 * half], d_low[2 * half :]], axis=1),
        ],
        axis=0,
    )
    staged = jnp.take(jnp.pad(child_local, ((0, 0), (0, 1))), col_send, axis=1)
    staged = lax.all_to_all(
        staged.reshape(child_rows, grid_cols, cap_cols), "pcol", split_axis=1, concat_axis=1, tiled=True
    ).reshape(child_rows, grid_cols * cap_cols)
    front_mat = front.reshape(local_rows, local_cols)
    staged, front_mat = lax.optimization_barrier((staged, front_mat))
    moved = jnp.take(jnp.pad(staged, ((0, 1), (0, 0))), row_send, axis=0)
    moved = lax.all_to_all(
        moved.reshape(grid_rows, cap_rows, grid_cols * cap_cols), "prow", split_axis=0, concat_axis=0, tiled=True
    )
    arrived = jnp.pad(moved.reshape(grid_rows * cap_rows, grid_cols * cap_cols), ((0, 1), (0, 1)))
    added = jnp.take(jnp.take(arrived, row_recv, axis=0), col_recv, axis=1)
    matrix = front_mat + added
    panel = NP * block_width
    row_blk = jnp.repeat(jnp.arange(row_blocks, dtype=jnp.int32) * grid_rows + my_row, block_width)
    col_blk = jnp.repeat(jnp.arange(col_blocks, dtype=jnp.int32) * grid_cols + my_col, block_width)
    first_cols = matrix[:, :block_width]
    first_rows = matrix[:block_width, :]
    zero_cols = jnp.zeros_like(first_cols)
    zero_rows = jnp.zeros_like(first_rows)
    x_part = jnp.concatenate(
        [jnp.where(my_col == p, first_cols, zero_cols) for p in range(NP)], axis=1
    )
    y_part = jnp.concatenate(
        [jnp.where(my_row == p, first_rows, zero_rows) for p in range(NP)], axis=0
    )
    d_full, x_part, y_part = lax.optimization_barrier((d_full, x_part, y_part))
    x_full = lax.psum(x_part, "pcol")
    y_full = lax.psum(y_part, "prow")
    low = jnp.tril(jnp.linalg.cholesky(d_full))
    low_inv = lower_inverse(low, min(128, panel))
    rows_f = jnp.dot(x_full, low_inv.T, precision=HIGHEST)
    cols_f = lax.dot_general(
        y_full, low_inv, (((0,), (1,)), ((), ())), precision=HIGHEST
    )
    low_rows = lax.dynamic_slice_in_dim(low, jnp.minimum(my_row, NP - 1) * block_width, block_width, 0)
    head = jnp.where(my_row < NP, low_rows, rows_f[:block_width])
    rows_f = jnp.concatenate([head, rows_f[block_width:]], axis=0)
    lane = jnp.arange(panel, dtype=jnp.int32)[None, :]
    keep_row = (row_blk[:, None] >= NP) | (lane < (row_blk[:, None] * block_width))
    rows_u = jnp.where(keep_row, rows_f, 0.0)
    cols_u = jnp.where((col_blk >= NP)[:, None], cols_f, 0.0)
    updated = matrix - jnp.dot(rows_u, cols_u.T, precision=HIGHEST)
    panel_src = jnp.where(my_col == 0, rows_f, jnp.roll(rows_f, -block_width, axis=1))
    out_lane = jnp.arange(local_cols, dtype=jnp.int32)[None, :]
    matrix = jnp.where((out_lane < block_width) & (my_col < NP), panel_src, updated)
    return matrix.reshape(front.shape)


def solution(mesh):
    in_specs = (
        P(None, "prow", None, None, "pcol", None),
        P(None, "prow", None, None, "pcol", None),
        P(),
    )
    out_specs = P(None, "prow", None, None, "pcol", None)
    return jax.shard_map(local, mesh=mesh, in_specs=in_specs, out_specs=out_specs, check_vma=False)
```
